128 devices in a mesh: shards: 8 (over x, core), tensor: 4 (over z), section: 4 (over y).
Axes of the slice: x: 4, y: 4, z: 4, core: 2. Of those that a mesh axis runs over, the one named last changes fastest.
Arguments:
- attn_grad: bfloat16 [16, 4, 1024, 1024], P('section', None, 'shards', 'tensor'), may hold values from -60 to 60
- mlp_in_grad: bfloat16 [16, 2, 1024, 2816], P('section', None, 'shards', 'tensor'), may hold values from -60 to 60
- mlp_out_grad: bfloat16 [16, 2816, 1024], P('section', 'tensor', 'shards'), may hold values from -60 to 60
- attn_momentum: bfloat16 [16, 4, 1024, 1024], P('section', None, 'shards', 'tensor'), may hold values from -3 to 3
- mlp_in_momentum: bfloat16 [16, 2, 1024, 2816], P('section', None, 'shards', 'tensor'), may hold values from -3 to 3
- mlp_out_momentum: bfloat16 [16, 2816, 1024], P('section', 'tensor', 'shards'), may hold values from -3 to 3
- owners: int32 [16, 7], P('section'), may hold values from 0 to 31, as said below
- embed_weight: float32 [32128, 1024], P(('shards', 'tensor', 'section')), may hold values from -6 to 6
- embed_grad: bfloat16 [32128, 1024], P(('shards', 'tensor', 'section')), may hold values from -6 to 6
- embed_moment: float32 [32128, 1024], P(('shards', 'tensor', 'section')), may hold values from -3 to 3
- embed_second: float32 [32128, 1024], P(('shards', 'tensor', 'section')), may hold values from 0.01 to 1
- norm_scale: float32 [16, 2048], P('section'), may hold values from 0.5 to 1.5
- norm_partial: float32 [16, 32, 2048], P('section', ('shards', 'tensor')), may hold values from -2 to 2
- norm_moment: float32 [16, 2048], P('section'), may hold values from -3 to 3
- norm_second: float32 [16, 2048], P('section'), may hold values from 0.01 to 0.5
- bias_table: float32 [32, 16], replicated, may hold values from -3 to 3
- bias_partial: float32 [128, 32, 16], P(('shards', 'tensor', 'section')), may hold values from -2 to 2
- bias_moment: float32 [32, 16], replicated, may hold values from -3 to 3
- bias_second: float32 [32, 16], replicated, may hold values from 0.01 to 1
Outputs:
- attn_momentum_new: bfloat16 [16, 4, 1024, 1024], P('section', None, 'shards', 'tensor')
- mlp_in_momentum_new: bfloat16 [16, 2, 1024, 2816], P('section', None, 'shards', 'tensor')
- mlp_out_momentum_new: bfloat16 [16, 2816, 1024], P('section', 'tensor', 'shards')
- attn_update: float32 [16, 4, 1024, 1024], P('section', None, 'shards', 'tensor')
- mlp_in_update: float32 [16, 2, 1024, 2816], P('section', None, 'shards', 'tensor')
- mlp_out_update: float32 [16, 2816, 1024], P('section', 'tensor', 'shards')
- owner_rms: float32 [128], P(('shards', 'tensor', 'section'))
- embed_weight_new: float32 [32128, 1024], P(('shards', 'tensor', 'section'))
- embed_moment_new: float32 [32128, 1024], P(('shards', 'tensor', 'section'))
- embed_second_new: float32 [32128, 1024], P(('shards', 'tensor', 'section'))
- norm_scale_new: float32 [16, 2048], P('section')
- norm_moment_new: float32 [16, 2048], P('section')
- norm_second_new: float32 [16, 2048], P('section')
- bias_table_new: float32 [32, 16], replicated
- bias_moment_new: float32 [32, 16], replicated
- bias_second_new: float32 [32, 16], replicated
The draws below stay inside these ranges and needn't reach their ends.
Inputs may be any that keep to these rules, and one draw needn't show every extreme that they name: Owner o names the device of index o among the 32 devices of the layer's section, in the order of the mesh (shards first); the 28 matrices of the layers of one section have distinct owners, so a device owns at most one matrix.
All inputs are finite; a program needn't handle non-finite values.
Results may differ from the reference program's by a relative error of at most 0.018.
Values may be sent and summed in bfloat16 or wider, within the bound.
No kernel may reach another device: no remote copies, remote signals or barrier semaphores. Data moves between devices by JAX's collectives and lax.ppermute only.
A program may use at most 192 MiB of HBM per device.

```python
import math
import jax
import jax.numpy as jnp
from jax import lax

D = 1024
FF = 2816
VOCAB = 32128
HEADS = 16
BUCKETS = 32
NS_STEPS = 2
GROUP = 32
LPS = 4
LAYERS = 16
N_SECTION = 4
DEVICES = 128


def rough_field(key, array_shape):
    key_noise, key_rows, key_cols = jax.random.split(key, 3)
    row_shape = array_shape[:-1] + (1,)
    col_shape = array_shape[:-2] + (1, array_shape[-1])
    row_scale = jnp.exp(jax.random.uniform(key_rows, row_shape, jnp.float32, math.log(0.3), math.log(3.0)))
    col_scale = jnp.exp(jax.random.uniform(key_cols, col_shape, jnp.float32, math.log(0.3), math.log(3.0)))
    noise_part = jnp.clip(jax.random.normal(key_noise, array_shape, jnp.float32), -5.0, 5.0)
    return noise_part * row_scale * col_scale


def draw_attn_grad(key, part):
    return rough_field(key, (LAYERS, 4, D, D)).astype(jnp.bfloat16)


def draw_mlp_in_grad(key, part):
    return rough_field(key, (LAYERS, 2, D, FF)).astype(jnp.bfloat16)


def draw_mlp_out_grad(key, part):
    return rough_field(key, (LAYERS, FF, D)).astype(jnp.bfloat16)


def draw_owners(key, part):
    section_keys = jax.random.split(key, LAYERS // LPS)
    chosen = jax.vmap(lambda section_key: jax.random.permutation(section_key, GROUP)[:7 * LPS])(section_keys)
    return chosen.reshape(LAYERS, 7).astype(jnp.int32)


def shard_levels(rng, extent, cuts, least, largest):
    level, own = 1.0, jax.random.fold_in(rng, 6)
    for dim, shards_of in cuts:
        draws = jnp.exp(jax.random.uniform(jax.random.fold_in(own, dim), (shards_of,), jnp.float32, least / len(cuts), largest / len(cuts)))
        level = level * jnp.repeat(draws, extent[dim] // shards_of).reshape([-1 if axis == dim else 1 for axis in range(len(extent))])
    return level


def gaussian(own_key, shape, spread, limit, shards=(), held_as=jnp.bfloat16):
    values = spread * jax.random.normal(own_key, shape, jnp.float32)
    if shards:
        values = values * shard_levels(own_key, shape, shards, -0.22, 0.18)
    return jnp.clip(values, -limit, limit).astype(held_as)


def setup_inputs(seed: int = 0) -> dict:
    seeds = jax.random.split(jax.random.key(seed), 20)
    attn_grad = draw_attn_grad(jax.random.fold_in(seeds[19], 71), 0)
    mlp_in_grad = draw_mlp_in_grad(jax.random.fold_in(seeds[19], 71), 0)
    mlp_out_grad = draw_mlp_out_grad(jax.random.fold_in(seeds[19], 71), 0)
    attn_momentum = gaussian(seeds[3], (LAYERS, 4, D, D), 0.5, 3.0, ((0, 4), (2, 8), (3, 4)))
    mlp_in_momentum = gaussian(seeds[4], (LAYERS, 2, D, FF), 0.5, 3.0, ((0, 4), (2, 8), (3, 4)))
    mlp_out_momentum = gaussian(seeds[5], (LAYERS, FF, D), 0.5, 3.0, ((0, 4), (1, 4), (2, 8)))
    owners = draw_owners(jax.random.fold_in(seeds[19], 71), 0)
    embed_weight = gaussian(seeds[7], (VOCAB, D), 1.0, 6.0, ((0, 128),), jnp.float32)
    embed_grad = gaussian(seeds[8], (VOCAB, D), 1.0, 6.0, ((0, 128),))
    embed_moment = gaussian(seeds[9], (VOCAB, D), 0.3, 3.0, ((0, 128),), jnp.float32)
    embed_second = jnp.clip(jnp.exp(math.log(1.0) - 4.6051702 * jax.random.uniform(seeds[10], (VOCAB, D), jnp.float32) ** shard_levels(seeds[10], (VOCAB, D), ((0, 128),), -0.2, 0.2)), 0.01, 1.0)
    norm_scale = jnp.clip(1.0 + 0.1 * jax.random.normal(seeds[11], (LAYERS, 2 * D), jnp.float32), 0.5, 1.5)
    norm_partial = gaussian(seeds[12], (LAYERS, GROUP, 2 * D), 0.25, 2.0, ((0, 4), (1, 32)), jnp.float32)
    norm_moment = gaussian(seeds[13], (LAYERS, 2 * D), 0.3, 3.0, ((0, 4),), jnp.float32)
    norm_second = jnp.clip(jnp.exp(math.log(0.5) - 3.912023 * jax.random.uniform(seeds[14], (LAYERS, 2 * D), jnp.float32) ** shard_levels(seeds[14], (LAYERS, 2 * D), ((0, 4),), -0.2, 0.2)), 0.01, 0.5)
    bias_table = gaussian(seeds[15], (BUCKETS, HEADS), 0.5, 3.0, (), jnp.float32)
    bias_partial = gaussian(seeds[16], (DEVICES, BUCKETS, HEADS), 0.25, 2.0, ((0, 128),), jnp.float32)
    bias_moment = gaussian(seeds[17], (BUCKETS, HEADS), 0.3, 3.0, (), jnp.float32)
    bias_second = jnp.clip(jnp.exp(jax.random.uniform(seeds[18], (BUCKETS, HEADS), jnp.float32, math.log(0.01), math.log(1.0))), 0.01, 1.0)
    return dict(attn_grad=attn_grad, mlp_in_grad=mlp_in_grad, mlp_out_grad=mlp_out_grad, attn_momentum=attn_momentum, mlp_in_momentum=mlp_in_momentum, mlp_out_momentum=mlp_out_momentum, owners=owners, embed_weight=embed_weight, embed_grad=embed_grad, embed_moment=embed_moment, embed_second=embed_second, norm_scale=norm_scale, norm_partial=norm_partial, norm_moment=norm_moment, norm_second=norm_second, bias_table=bias_table, bias_partial=bias_partial, bias_moment=bias_moment, bias_second=bias_second)


coef_first = 3.4445
coef_second = -4.775
coef_third = 2.0315

def orthogonalize(matrix):
    norm_value = jnp.sqrt(jnp.sum(matrix * matrix))
    current = (matrix / (norm_value + 1e-07)).astype(jnp.bfloat16)
    for sweep_index in range(NS_STEPS):
        gram_form = jnp.dot(current, current.T, preferred_element_type=jnp.float32).astype(jnp.bfloat16)
        square_form = jnp.dot(gram_form, gram_form, preferred_element_type=jnp.float32)
        polynomial = (coef_second * gram_form.astype(jnp.float32) + coef_third * square_form).astype(jnp.bfloat16)
        current = (coef_first * current.astype(jnp.float32) + jnp.dot(polynomial, current, preferred_element_type=jnp.float32)).astype(jnp.bfloat16)
    final_scale = 0.2 * math.sqrt(max(matrix.shape[0], matrix.shape[1]))
    rms_value = norm_value / math.sqrt(matrix.shape[0] * matrix.shape[1])
    return (current.astype(jnp.float32) * final_scale, rms_value)

def refresh(gradient, moment):
    fresh_moment = (0.95 * moment.astype(jnp.float32) + gradient.astype(jnp.float32)).astype(jnp.bfloat16)
    advance = (gradient.astype(jnp.float32) + 0.95 * fresh_moment.astype(jnp.float32)).astype(jnp.bfloat16)
    return (fresh_moment, advance)

def adamw_update(weight, gradient, moment, second, decay_rate):
    moment_new = 0.9 * moment + 0.1 * gradient
    second_new = 0.95 * second + 0.05 * gradient * gradient
    weight_new = weight - 0.02 * (moment_new / (jnp.sqrt(second_new) + 1e-08) + decay_rate * weight)
    return (weight_new, moment_new, second_new)

def one_layer(inputs):
    square_ahead, inner_ahead, outer_ahead = inputs
    square_list = []
    inner_list = []
    rms_list = []
    for position in range(4):
        update_part, rms_value = orthogonalize(square_ahead[position].astype(jnp.float32))
        square_list.append(update_part)
        rms_list.append(rms_value)
    for position in range(2):
        update_part, rms_value = orthogonalize(inner_ahead[position].astype(jnp.float32))
        inner_list.append(update_part)
        rms_list.append(rms_value)
    update_part, rms_value = orthogonalize(outer_ahead.T.astype(jnp.float32))
    rms_list.append(rms_value)
    return (jnp.stack(square_list), jnp.stack(inner_list), update_part.T, jnp.stack(rms_list))

def reference(attn_grad, mlp_in_grad, mlp_out_grad, attn_momentum, mlp_in_momentum, mlp_out_momentum, owners, embed_weight, embed_grad, embed_moment, embed_second, norm_scale, norm_partial, norm_moment, norm_second, bias_table, bias_partial, bias_moment, bias_second):
    attn_fresh, attn_ahead = refresh(attn_grad, attn_momentum)
    inner_fresh, inner_ahead = refresh(mlp_in_grad, mlp_in_momentum)
    outer_fresh, outer_ahead = refresh(mlp_out_grad, mlp_out_momentum)
    attn_update, mlp_in_update, mlp_out_update, rms_table = lax.map(one_layer, (attn_ahead, inner_ahead, outer_ahead))
    section_index = jnp.arange(LAYERS, dtype=jnp.int32) // LPS
    positions = (owners * N_SECTION + section_index[:, None]).astype(jnp.int32)
    owner_rms = jnp.zeros((DEVICES,), jnp.float32).at[positions.reshape(-1)].set(rms_table.reshape(-1))
    embed_results = adamw_update(embed_weight, embed_grad.astype(jnp.float32), embed_moment, embed_second, 0.1)
    norm_grad = lax.optimization_barrier(jnp.sum(norm_partial, axis=1))
    norm_results = adamw_update(norm_scale, norm_grad, norm_moment, norm_second, 0.0)
    bias_grad = lax.optimization_barrier(jnp.sum(bias_partial, axis=0))
    bias_results = adamw_update(bias_table, bias_grad, bias_moment, bias_second, 0.0)
    return (attn_fresh, inner_fresh, outer_fresh, attn_update, mlp_in_update, mlp_out_update, owner_rms, embed_results[0], embed_results[1], embed_results[2], norm_results[0], norm_results[1], norm_results[2], bias_results[0], bias_results[1], bias_results[2])
```

```python
import math

import jax
import jax.numpy as jnp
from jax import lax
from jax.sharding import PartitionSpec as P

D = 1024
FF = 2816
NS_STEPS = 2


coef_first = 3.4445
coef_second = -4.775
coef_third = 2.0315


def orthogonalize(matrix):
    norm_value = jnp.sqrt(jnp.sum(matrix * matrix))
    current = (matrix / (norm_value + 1e-07)).astype(jnp.bfloat16)
    for sweep_index in range(NS_STEPS):
        gram_form = jnp.dot(current, current.T, preferred_element_type=jnp.float32).astype(
            jnp.bfloat16
        )
        square_form = jnp.dot(gram_form, gram_form, preferred_element_type=jnp.float32)
        polynomial = (
            coef_second * gram_form.astype(jnp.float32) + coef_third * square_form
        ).astype(jnp.bfloat16)
        current = (
            coef_first * current.astype(jnp.float32)
            + jnp.dot(polynomial, current, preferred_element_type=jnp.float32)
        ).astype(jnp.bfloat16)
    rms_value = norm_value / math.sqrt(matrix.shape[0] * matrix.shape[1])
    return (current, rms_value)


def refresh(gradient, moment):
    fresh_moment = (0.95 * moment.astype(jnp.float32) + gradient.astype(jnp.float32)).astype(
        jnp.bfloat16
    )
    advance = (gradient.astype(jnp.float32) + 0.95 * fresh_moment.astype(jnp.float32)).astype(
        jnp.bfloat16
    )
    return (fresh_moment, advance)


def adamw_update(weight, gradient, moment, second, decay_rate):
    moment_new = 0.9 * moment + 0.1 * gradient
    second_new = 0.95 * second + 0.05 * gradient * gradient
    weight_new = weight - 0.02 * (moment_new / (jnp.sqrt(second_new) + 1e-08) + decay_rate * weight)
    return (weight_new, moment_new, second_new)


def on_device(
    attn_grad,
    mlp_in_grad,
    mlp_out_grad,
    attn_momentum,
    mlp_in_momentum,
    mlp_out_momentum,
    owners,
    embed_weight,
    embed_grad,
    embed_moment,
    embed_second,
    norm_scale,
    norm_partial,
    norm_moment,
    norm_second,
    bias_table,
    bias_partial,
    bias_moment,
    bias_second,
):
    shards_count = lax.axis_size("shards")
    tensor_count = lax.axis_size("tensor")
    group_count = shards_count * tensor_count
    my_index = lax.axis_index(("shards", "tensor"))
    layers_here = owners.shape[0]
    rows_block = attn_grad.shape[2]
    cols_block = attn_grad.shape[3]
    ff_block = mlp_in_grad.shape[3]
    square_width = rows_block * cols_block
    rect_width = rows_block * ff_block
    slot_width = max(square_width, rect_width)

    norm_all = lax.all_gather(norm_partial[:, 0], ("shards", "tensor"), axis=0, tiled=False)
    bias_all = lax.all_gather(bias_partial[0], ("shards", "tensor", "section"), axis=0, tiled=False)
    norm_grad = jnp.sum(norm_all, axis=0)
    bias_grad = jnp.sum(bias_all, axis=0)

    attn_fresh, attn_ahead = refresh(attn_grad, attn_momentum)
    inner_fresh, inner_ahead = refresh(mlp_in_grad, mlp_in_momentum)
    outer_fresh, outer_ahead = refresh(mlp_out_grad, mlp_out_momentum)
    rect_ahead = jnp.concatenate([inner_ahead, jnp.swapaxes(outer_ahead, 1, 2)[:, None]], axis=1)

    slots = jnp.arange(group_count, dtype=jnp.int32)
    square_owner = owners[:, :4].reshape(-1)
    rect_owner = owners[:, 4:].reshape(-1)
    square_pick = (slots[:, None] == square_owner[None, :]).astype(jnp.bfloat16)
    rect_pick = (slots[:, None] == rect_owner[None, :]).astype(jnp.bfloat16)
    square_send = jnp.dot(
        square_pick,
        attn_ahead.reshape(layers_here * 4, square_width),
        preferred_element_type=jnp.float32,
    )
    rect_send = jnp.dot(
        rect_pick,
        rect_ahead.reshape(layers_here * 3, rect_width),
        preferred_element_type=jnp.float32,
    )
    outgoing = (
        jnp.pad(square_send, ((0, 0), (0, slot_width - square_width))) + rect_send
    ).astype(jnp.bfloat16)
    incoming = lax.all_to_all(outgoing, ("shards", "tensor"), split_axis=0, concat_axis=0, tiled=True)

    def square_branch(arrived_blocks):
        whole = (
            arrived_blocks[:, :square_width]
            .astype(jnp.float32)
            .reshape(shards_count, tensor_count, rows_block, cols_block)
            .transpose(0, 2, 1, 3)
            .reshape(shards_count * rows_block, tensor_count * cols_block)
        )
        done, rms = orthogonalize(whole)
        back = (
            done.reshape(shards_count, rows_block, tensor_count, cols_block)
            .transpose(0, 2, 1, 3)
            .reshape(group_count, square_width)
        )
        return jnp.pad(back, ((0, 0), (0, slot_width - square_width))), rms

    def rect_branch(arrived_blocks):
        whole = (
            arrived_blocks[:, :rect_width]
            .astype(jnp.float32)
            .reshape(shards_count, tensor_count, rows_block, ff_block)
            .transpose(0, 2, 1, 3)
            .reshape(shards_count * rows_block, tensor_count * ff_block)
        )
        done, rms = orthogonalize(whole)
        back = (
            done.reshape(shards_count, rows_block, tensor_count, ff_block)
            .transpose(0, 2, 1, 3)
            .reshape(group_count, rect_width)
        )
        return jnp.pad(back, ((0, 0), (0, slot_width - rect_width))), rms

    def idle_branch(arrived_blocks):
        return jnp.zeros((group_count, slot_width), jnp.bfloat16), jnp.zeros((), jnp.float32)

    owns_square = jnp.any(square_owner == my_index)
    owns_rect = jnp.any(rect_owner == my_index)
    kind = jnp.where(owns_rect, 2, jnp.where(owns_square, 1, 0)).astype(jnp.int32)
    returning, my_rms = lax.switch(kind, [idle_branch, square_branch, rect_branch], incoming)

    arrived = lax.all_to_all(returning, ("shards", "tensor"), split_axis=0, concat_axis=0, tiled=True)
    square_rows = (
        jnp.dot(square_pick.T, arrived[:, :square_width], preferred_element_type=jnp.float32)
        .reshape(layers_here, 4, rows_block, cols_block)
        * (0.2 * math.sqrt(D))
    )
    rect_rows = jnp.dot(rect_pick.T, arrived[:, :rect_width], preferred_element_type=jnp.float32).reshape(
        layers_here, 3, rows_block, ff_block
    ) * (0.2 * math.sqrt(FF))
    mlp_in_update = rect_rows[:, :2]
    mlp_out_update = jnp.swapaxes(rect_rows[:, 2], 1, 2)
    owner_rms = my_rms.reshape(1)

    embed_results = adamw_update(
        embed_weight, embed_grad.astype(jnp.float32), embed_moment, embed_second, 0.1
    )
    norm_results = adamw_update(norm_scale, norm_grad, norm_moment, norm_second, 0.0)
    bias_results = adamw_update(bias_table, bias_grad, bias_moment, bias_second, 0.0)
    return (
        attn_fresh,
        inner_fresh,
        outer_fresh,
        square_rows,
        mlp_in_update,
        mlp_out_update,
        owner_rms,
        embed_results[0],
        embed_results[1],
        embed_results[2],
        norm_results[0],
        norm_results[1],
        norm_results[2],
        bias_results[0],
        bias_results[1],
        bias_results[2],
    )


def solution(mesh):
    placed = (
        P("section", None, "shards", "tensor"),
        P("section", None, "shards", "tensor"),
        P("section", "tensor", "shards"),
        P("section", None, "shards", "tensor"),
        P("section", None, "shards", "tensor"),
        P("section", "tensor", "shards"),
        P("section", None),
        P(("shards", "tensor", "section"), None),
        P(("shards", "tensor", "section"), None),
        P(("shards", "tensor", "section"), None),
        P(("shards", "tensor", "section"), None),
        P("section", None),
        P("section", ("shards", "tensor"), None),
        P("section", None),
        P("section", None),
        P(),
        P(("shards", "tensor", "section"), None, None),
        P(),
        P(),
    )
    return jax.shard_map(
        on_device,
        mesh=mesh,
        in_specs=placed,
        out_specs=(
            P("section", None, "shards", "tensor"),
            P("section", None, "shards", "tensor"),
            P("section", "tensor", "shards"),
            P("section", None, "shards", "tensor"),
            P("section", None, "shards", "tensor"),
            P("section", "tensor", "shards"),
            P(("shards", "tensor", "section")),
            P(("shards", "tensor", "section"), None),
            P(("shards", "tensor", "section"), None),
            P(("shards", "tensor", "section"), None),
            P("section", None),
            P("section", None),
            P("section", None),
            P(),
            P(),
            P(),
        ),
        check_vma=False,
    )
```

```python
import math

import jax
import jax.numpy as jnp
from jax import lax
from jax.sharding import PartitionSpec as P

D = 1024
FF = 2816
NS_STEPS = 2


coef_first = 3.4445
coef_second = -4.775
coef_third = 2.0315


def newton_schulz(blocks_bf16, norm_value):
    current = (blocks_bf16.astype(jnp.float32) / (norm_value + 1e-07)).astype(jnp.bfloat16)
    for sweep_index in range(NS_STEPS):
        gram_form = jnp.dot(current, current.T, preferred_element_type=jnp.float32).astype(
            jnp.bfloat16
        )
        square_form = jnp.dot(gram_form, gram_form, preferred_element_type=jnp.float32)
        polynomial = (
            coef_second * gram_form.astype(jnp.float32) + coef_third * square_form
        ).astype(jnp.bfloat16)
        current = (
            coef_first * current.astype(jnp.float32)
            + jnp.dot(polynomial, current, preferred_element_type=jnp.float32)
        ).astype(jnp.bfloat16)
    return current


def refresh(gradient, moment):
    fresh_moment = (0.95 * moment.astype(jnp.float32) + gradient.astype(jnp.float32)).astype(
        jnp.bfloat16
    )
    advance = (gradient.astype(jnp.float32) + 0.95 * fresh_moment.astype(jnp.float32)).astype(
        jnp.bfloat16
    )
    return (fresh_moment, advance)


def adamw_update(weight, gradient, moment, second, decay_rate):
    moment_new = 0.9 * moment + 0.1 * gradient
    second_new = 0.95 * second + 0.05 * gradient * gradient
    weight_new = weight - 0.02 * (moment_new / (jnp.sqrt(second_new) + 1e-08) + decay_rate * weight)
    return (weight_new, moment_new, second_new)


def block_plan(shards_count, tensor_count):
    kind = [0] * (shards_count * tensor_count)
    index = [0] * (shards_count * tensor_count)
    chips = [(x, z) for x in range(shards_count // 2) for z in range(tensor_count)]
    for number, (x, z) in enumerate(chips):
        kind[(2 * x + 1) * tensor_count + z] = 1
        index[(2 * x + 1) * tensor_count + z] = number
    for number, (x, z) in enumerate(chips[:12]):
        kind[(2 * x) * tensor_count + z] = 2
        index[(2 * x) * tensor_count + z] = number
    return kind, index


def on_device(
    attn_grad,
    mlp_in_grad,
    mlp_out_grad,
    attn_momentum,
    mlp_in_momentum,
    mlp_out_momentum,
    owners,
    embed_weight,
    embed_grad,
    embed_moment,
    embed_second,
    norm_scale,
    norm_partial,
    norm_moment,
    norm_second,
    bias_table,
    bias_partial,
    bias_moment,
    bias_second,
):
    shards_count = lax.axis_size("shards")
    tensor_count = lax.axis_size("tensor")
    group_count = shards_count * tensor_count
    my_index = lax.axis_index(("shards", "tensor"))
    my_row = my_index // tensor_count
    my_col = my_index % tensor_count
    layers_here = owners.shape[0]
    rows_block = attn_grad.shape[2]
    cols_block = attn_grad.shape[3]
    ff_block = mlp_in_grad.shape[3]
    square_width = rows_block * cols_block
    rect_width = rows_block * ff_block
    n_square = layers_here * 4
    n_rect = layers_here * 3
    kind_list, index_list = block_plan(shards_count, tensor_count)
    assert sum(k == 1 for k in kind_list) == n_square and sum(k == 2 for k in kind_list) == n_rect
    kind_table = jnp.array(kind_list, jnp.int32)
    index_table = jnp.array(index_list, jnp.int32)
    square_home = [0] * n_square
    rect_home = [0] * n_rect
    for device, (k, i) in enumerate(zip(kind_list, index_list)):
        if k == 1:
            square_home[i] = device
        elif k == 2:
            rect_home[i] = device

    attn_fresh, attn_ahead = refresh(attn_grad, attn_momentum)
    inner_fresh, inner_ahead = refresh(mlp_in_grad, mlp_in_momentum)
    outer_fresh, outer_ahead = refresh(mlp_out_grad, mlp_out_momentum)
    square_table = attn_ahead.reshape(n_square, rows_block, cols_block)
    rect_table = jnp.concatenate(
        [inner_ahead, jnp.swapaxes(outer_ahead, 1, 2)[:, None]], axis=1
    ).reshape(n_rect, rows_block, ff_block)

    square_ss = jnp.sum(jnp.square(square_table.astype(jnp.float32)), axis=(1, 2))
    rect_ss = jnp.sum(jnp.square(rect_table.astype(jnp.float32)), axis=(1, 2))
    norm_width = norm_partial.shape[0] * norm_partial.shape[2]
    packed = jnp.concatenate([norm_partial.reshape(norm_width), square_ss, rect_ss])
    packed = jnp.pad(packed, (0, (-packed.shape[0]) % 128))
    gathered = jnp.sum(lax.all_gather(packed, ("shards", "tensor"), axis=0, tiled=False), axis=0)
    norm_grad = gathered[:norm_width].reshape(norm_partial.shape[0], norm_partial.shape[2])
    square_norm = jnp.sqrt(gathered[norm_width : norm_width + n_square])
    rect_norm = jnp.sqrt(gathered[norm_width + n_square : norm_width + n_square + n_rect])
    bias_flat = bias_partial.reshape(-1)
    bias_pad = jnp.pad(bias_flat, (0, 2048 - bias_flat.shape[0]))
    bias_all = lax.all_gather(bias_pad, ("shards", "tensor", "section"), axis=0, tiled=False)
    bias_grad = jnp.sum(bias_all, axis=0)[: bias_flat.shape[0]].reshape(bias_table.shape)

    rms_all = jnp.concatenate(
        [
            square_norm.reshape(layers_here, 4) / math.sqrt(D * D),
            rect_norm.reshape(layers_here, 3) / math.sqrt(D * FF),
        ],
        axis=1,
    )
    owner_rms = jnp.sum(jnp.where(owners == my_index, rms_all, 0.0)).reshape(1)

    shifts = [(a, b) for a in range(shards_count) for b in range(tensor_count)]
    step_a = jnp.array([a for a, b in shifts], jnp.int32)
    step_b = jnp.array([b for a, b in shifts], jnp.int32)
    dest = ((my_row + step_a) % shards_count) * tensor_count + (my_col + step_b) % tensor_count
    dest_kind = kind_table[dest]
    dest_index = index_table[dest]
    square_rot = jnp.dot(
        ((dest_kind == 1)[:, None] & (dest_index[:, None] == jnp.arange(n_square)[None, :])).astype(
            jnp.bfloat16
        ),
        square_table.reshape(n_square, square_width),
        preferred_element_type=jnp.float32,
    ).astype(jnp.bfloat16)
    rect_rot = jnp.dot(
        ((dest_kind == 2)[:, None] & (dest_index[:, None] == jnp.arange(n_rect)[None, :])).astype(
            jnp.bfloat16
        ),
        rect_table.reshape(n_rect, rect_width),
        preferred_element_type=jnp.float32,
    ).astype(jnp.bfloat16)

    def shift_pairs(a, b, sign, wanted, by_dest):
        pairs = []
        for s in range(shards_count):
            for t in range(tensor_count):
                src = s * tensor_count + t
                dst = ((s + sign * a) % shards_count) * tensor_count + (t + sign * b) % tensor_count
                if kind_list[dst if by_dest else src] == wanted:
                    pairs.append((src, dst))
        return pairs

    square_in = [square_rot[0]]
    rect_in = [rect_rot[0]]
    for k, (a, b) in enumerate(shifts[1:], start=1):
        square_in.append(
            lax.ppermute(square_rot[k], ("shards", "tensor"), shift_pairs(a, b, 1, 1, True))
        )
        rect_in.append(lax.ppermute(rect_rot[k], ("shards", "tensor"), shift_pairs(a, b, 1, 2, True)))

    def assemble(blocks, width):
        rows = [
            jnp.concatenate(blocks[a * tensor_count : (a + 1) * tensor_count], axis=1).reshape(
                rows_block, tensor_count * width
            )
            for a in range(shards_count)
        ]
        return jnp.concatenate(rows, axis=0)

    def run(blocks, width, norm_value):
        whole = assemble([x.reshape(rows_block, width) for x in blocks], width)
        done = newton_schulz(whole, norm_value)
        return [
            done[a * rows_block : (a + 1) * rows_block, b * width : (b + 1) * width]
            for a, b in shifts
        ]

    my_kind = kind_table[my_index]
    my_mat = index_table[my_index]

    def square_branch(operands):
        square_blocks, rect_blocks = operands
        out = run(square_blocks, cols_block, square_norm[my_mat])
        return jnp.stack(out), jnp.zeros((group_count, rows_block, ff_block), jnp.bfloat16)

    def rect_branch(operands):
        square_blocks, rect_blocks = operands
        out = run(rect_blocks, ff_block, rect_norm[my_mat])
        return jnp.zeros((group_count, rows_block, cols_block), jnp.bfloat16), jnp.stack(out)

    def idle_branch(operands):
        return (
            jnp.zeros((group_count, rows_block, cols_block), jnp.bfloat16),
            jnp.zeros((group_count, rows_block, ff_block), jnp.bfloat16),
        )

    square_done, rect_done = lax.switch(
        my_kind, [idle_branch, square_branch, rect_branch], (square_in, rect_in)
    )

    square_back = [square_done[0]]
    rect_back = [rect_done[0]]
    for k, (a, b) in enumerate(shifts[1:], start=1):
        square_back.append(
            lax.ppermute(square_done[k], ("shards", "tensor"), shift_pairs(a, b, -1, 1, False))
        )
        rect_back.append(
            lax.ppermute(rect_done[k], ("shards", "tensor"), shift_pairs(a, b, -1, 2, False))
        )
    square_back = jnp.stack(square_back).reshape(group_count, square_width)
    rect_back = jnp.stack(rect_back).reshape(group_count, rect_width)

    def arrival_round(home):
        home = jnp.array(home, jnp.int32)
        a = (home // tensor_count - my_row) % shards_count
        b = (home % tensor_count - my_col) % tensor_count
        return a * tensor_count + b

    square_pick = (
        arrival_round(square_home)[:, None] == jnp.arange(group_count)[None, :]
    ).astype(jnp.bfloat16)
    rect_pick = (arrival_round(rect_home)[:, None] == jnp.arange(group_count)[None, :]).astype(
        jnp.bfloat16
    )
    square_rows = jnp.dot(square_pick, square_back, preferred_element_type=jnp.float32).reshape(
        layers_here, 4, rows_block, cols_block
    ) * (0.2 * math.sqrt(D))
    rect_rows = jnp.dot(rect_pick, rect_back, preferred_element_type=jnp.float32).reshape(
        layers_here, 3, rows_block, ff_block
    ) * (0.2 * math.sqrt(FF))
    mlp_in_update = rect_rows[:, :2]
    mlp_out_update = jnp.swapaxes(rect_rows[:, 2], 1, 2)

    embed_results = adamw_update(
        embed_weight, embed_grad.astype(jnp.float32), embed_moment, embed_second, 0.1
    )
    norm_results = adamw_update(norm_scale, norm_grad, norm_moment, norm_second, 0.0)
    bias_results = adamw_update(bias_table, bias_grad, bias_moment, bias_second, 0.0)
    return (
        attn_fresh,
        inner_fresh,
        outer_fresh,
        square_rows,
        mlp_in_update,
        mlp_out_update,
        owner_rms,
        embed_results[0],
        embed_results[1],
        embed_results[2],
        norm_results[0],
        norm_results[1],
        norm_results[2],
        bias_results[0],
        bias_results[1],
        bias_results[2],
    )


def solution(mesh):
    placed = (
        P("section", None, "shards", "tensor"),
        P("section", None, "shards", "tensor"),
        P("section", "tensor", "shards"),
        P("section", None, "shards", "tensor"),
        P("section", None, "shards", "tensor"),
        P("section", "tensor", "shards"),
        P("section", None),
        P(("shards", "tensor", "section"), None),
        P(("shards", "tensor", "section"), None),
        P(("shards", "tensor", "section"), None),
        P(("shards", "tensor", "section"), None),
        P("section", None),
        P("section", ("shards", "tensor"), None),
        P("section", None),
        P("section", None),
        P(),
        P(("shards", "tensor", "section"), None, None),
        P(),
        P(),
    )
    return jax.shard_map(
        on_device,
        mesh=mesh,
        in_specs=placed,
        out_specs=(
            P("section", None, "shards", "tensor"),
            P("section", None, "shards", "tensor"),
            P("section", "tensor", "shards"),
            P("section", None, "shards", "tensor"),
            P("section", None, "shards", "tensor"),
            P("section", "tensor", "shards"),
            P(("shards", "tensor", "section")),
            P(("shards", "tensor", "section"), None),
            P(("shards", "tensor", "section"), None),
            P(("shards", "tensor", "section"), None),
            P("section", None),
            P("section", None),
            P("section", None),
            P(),
            P(),
            P(),
        ),
        check_vma=False,
    )
```

```python
import math

import jax
import jax.numpy as jnp
from jax import lax
from jax.sharding import PartitionSpec as P

D = 1024
FF = 2816
NS_STEPS = 2


coef_first = 3.4445
coef_second = -4.775
coef_third = 2.0315


def newton_schulz(blocks_bf16, norm_value):
    current = (blocks_bf16.astype(jnp.float32) / (norm_value + 1e-07)).astype(jnp.bfloat16)
    for sweep_index in range(NS_STEPS):
        gram_form = jnp.dot(current, current.T, preferred_element_type=jnp.float32).astype(
            jnp.bfloat16
        )
        square_form = jnp.dot(gram_form, gram_form, preferred_element_type=jnp.float32)
        polynomial = (
            coef_second * gram_form.astype(jnp.float32) + coef_third * square_form
        ).astype(jnp.bfloat16)
        current = (
            coef_first * current.astype(jnp.float32)
            + jnp.dot(polynomial, current, preferred_element_type=jnp.float32)
        ).astype(jnp.bfloat16)
    return current


def refresh(gradient, moment):
    fresh_moment = (0.95 * moment.astype(jnp.float32) + gradient.astype(jnp.float32)).astype(
        jnp.bfloat16
    )
    advance = (gradient.astype(jnp.float32) + 0.95 * fresh_moment.astype(jnp.float32)).astype(
        jnp.bfloat16
    )
    return (fresh_moment, advance)


def adamw_update(weight, gradient, moment, second, decay_rate):
    moment_new = 0.9 * moment + 0.1 * gradient
    second_new = 0.95 * second + 0.05 * gradient * gradient
    weight_new = weight - 0.02 * (moment_new / (jnp.sqrt(second_new) + 1e-08) + decay_rate * weight)
    return (weight_new, moment_new, second_new)


def block_plan(shards_count, tensor_count):
    kind = [0] * (shards_count * tensor_count)
    index = [0] * (shards_count * tensor_count)
    chips = [(x, z) for x in range(shards_count // 2) for z in range(tensor_count)]
    for number, (x, z) in enumerate(chips):
        kind[(2 * x + 1) * tensor_count + z] = 1
        index[(2 * x + 1) * tensor_count + z] = number
    for number, (x, z) in enumerate(chips[:12]):
        kind[(2 * x) * tensor_count + z] = 2
        index[(2 * x) * tensor_count + z] = number
    return kind, index


def on_device(
    attn_grad,
    mlp_in_grad,
    mlp_out_grad,
    attn_momentum,
    mlp_in_momentum,
    mlp_out_momentum,
    owners,
    embed_weight,
    embed_grad,
    embed_moment,
    embed_second,
    norm_scale,
    norm_partial,
    norm_moment,
    norm_second,
    bias_table,
    bias_partial,
    bias_moment,
    bias_second,
):
    shards_count = lax.axis_size("shards")
    tensor_count = lax.axis_size("tensor")
    group_count = shards_count * tensor_count
    my_index = lax.axis_index(("shards", "tensor"))
    my_row = my_index // tensor_count
    my_col = my_index % tensor_count
    layers_here = owners.shape[0]
    rows_block = attn_grad.shape[2]
    cols_block = attn_grad.shape[3]
    ff_block = mlp_in_grad.shape[3]
    square_width = rows_block * cols_block
    rect_width = rows_block * ff_block
    n_square = layers_here * 4
    n_rect = layers_here * 3
    kind_list, index_list = block_plan(shards_count, tensor_count)
    assert sum(k == 1 for k in kind_list) == n_square and sum(k == 2 for k in kind_list) == n_rect
    kind_table = jnp.array(kind_list, jnp.int32)
    index_table = jnp.array(index_list, jnp.int32)
    square_home = [0] * n_square
    rect_home = [0] * n_rect
    for device, (k, i) in enumerate(zip(kind_list, index_list)):
        if k == 1:
            square_home[i] = device
        elif k == 2:
            rect_home[i] = device

    attn_fresh, attn_ahead = refresh(attn_grad, attn_momentum)
    inner_fresh, inner_ahead = refresh(mlp_in_grad, mlp_in_momentum)
    outer_fresh, outer_ahead = refresh(mlp_out_grad, mlp_out_momentum)
    square_table = attn_ahead.reshape(n_square, rows_block, cols_block)
    rect_table = jnp.concatenate(
        [inner_ahead, jnp.swapaxes(outer_ahead, 1, 2)[:, None]], axis=1
    ).reshape(n_rect, rows_block, ff_block)

    square_ss = jnp.sum(jnp.square(square_table.astype(jnp.float32)), axis=(1, 2))
    rect_ss = jnp.sum(jnp.square(rect_table.astype(jnp.float32)), axis=(1, 2))
    norm_width = norm_partial.shape[0] * norm_partial.shape[2]
    packed = jnp.concatenate([norm_partial.reshape(norm_width), square_ss, rect_ss])
    packed = jnp.pad(packed, (0, (-packed.shape[0]) % 128))
    gathered = jnp.sum(lax.all_gather(packed, ("shards", "tensor"), axis=0, tiled=False), axis=0)
    norm_grad = gathered[:norm_width].reshape(norm_partial.shape[0], norm_partial.shape[2])
    square_norm = jnp.sqrt(gathered[norm_width : norm_width + n_square])
    rect_norm = jnp.sqrt(gathered[norm_width + n_square : norm_width + n_square + n_rect])
    bias_flat = bias_partial.reshape(-1)
    bias_pad = jnp.pad(bias_flat, (0, 2048 - bias_flat.shape[0]))
    bias_all = lax.all_gather(bias_pad, ("shards", "tensor", "section"), axis=0, tiled=False)
    bias_grad = jnp.sum(bias_all, axis=0)[: bias_flat.shape[0]].reshape(bias_table.shape)

    rms_all = jnp.concatenate(
        [
            square_norm.reshape(layers_here, 4) / math.sqrt(D * D),
            rect_norm.reshape(layers_here, 3) / math.sqrt(D * FF),
        ],
        axis=1,
    )
    owner_rms = jnp.sum(jnp.where(owners == my_index, rms_all, 0.0)).reshape(1)

    def padded(block):
        return jnp.pad(block, ((0, 0), (0, ff_block - block.shape[1])))

    zero_slot = jnp.zeros((rows_block, ff_block), jnp.bfloat16)
    slots_out = []
    for device in range(group_count):
        if kind_list[device] == 1:
            slots_out.append(padded(square_table[index_list[device]]))
        elif kind_list[device] == 2:
            slots_out.append(rect_table[index_list[device]])
        else:
            slots_out.append(zero_slot)
    outgoing = jnp.stack(slots_out)
    incoming = lax.all_to_all(outgoing, ("shards", "tensor"), split_axis=0, concat_axis=0, tiled=True)

    def run(arrived_blocks, width, norm_value):
        whole = (
            arrived_blocks[:, :, :width]
            .reshape(shards_count, tensor_count, rows_block, width)
            .transpose(0, 2, 1, 3)
            .reshape(shards_count * rows_block, tensor_count * width)
        )
        done = newton_schulz(whole, norm_value)
        back = (
            done.reshape(shards_count, rows_block, tensor_count, width)
            .transpose(0, 2, 1, 3)
            .reshape(group_count, rows_block, width)
        )
        return jnp.pad(back, ((0, 0), (0, 0), (0, ff_block - width)))

    my_kind = kind_table[my_index]
    my_mat = index_table[my_index]

    def square_branch(arrived_blocks):
        return run(arrived_blocks, cols_block, square_norm[my_mat])

    def rect_branch(arrived_blocks):
        return run(arrived_blocks, ff_block, rect_norm[my_mat])

    def idle_branch(arrived_blocks):
        return jnp.zeros((group_count, rows_block, ff_block), jnp.bfloat16)

    returning = lax.switch(my_kind, [idle_branch, square_branch, rect_branch], incoming)
    arrived = lax.all_to_all(returning, ("shards", "tensor"), split_axis=0, concat_axis=0, tiled=True)

    square_rows = jnp.stack([arrived[device, :, :cols_block] for device in square_home]).reshape(
        layers_here, 4, rows_block, cols_block
    ).astype(jnp.float32) * (0.2 * math.sqrt(D))
    rect_rows = jnp.stack([arrived[device] for device in rect_home]).reshape(
        layers_here, 3, rows_block, ff_block
    ).astype(jnp.float32) * (0.2 * math.sqrt(FF))
    mlp_in_update = rect_rows[:, :2]
    mlp_out_update = jnp.swapaxes(rect_rows[:, 2], 1, 2)

    embed_results = adamw_update(
        embed_weight, embed_grad.astype(jnp.float32), embed_moment, embed_second, 0.1
    )
    norm_results = adamw_update(norm_scale, norm_grad, norm_moment, norm_second, 0.0)
    bias_results = adamw_update(bias_table, bias_grad, bias_moment, bias_second, 0.0)
    return (
        attn_fresh,
        inner_fresh,
        outer_fresh,
        square_rows,
        mlp_in_update,
        mlp_out_update,
        owner_rms,
        embed_results[0],
        embed_results[1],
        embed_results[2],
        norm_results[0],
        norm_results[1],
        norm_results[2],
        bias_results[0],
        bias_results[1],
        bias_results[2],
    )


def solution(mesh):
    placed = (
        P("section", None, "shards", "tensor"),
        P("section", None, "shards", "tensor"),
        P("section", "tensor", "shards"),
        P("section", None, "shards", "tensor"),
        P("section", None, "shards", "tensor"),
        P("section", "tensor", "shards"),
        P("section", None),
        P(("shards", "tensor", "section"), None),
        P(("shards", "tensor", "section"), None),
        P(("shards", "tensor", "section"), None),
        P(("shards", "tensor", "section"), None),
        P("section", None),
        P("section", ("shards", "tensor"), None),
        P("section", None),
        P("section", None),
        P(),
        P(("shards", "tensor", "section"), None, None),
        P(),
        P(),
    )
    return jax.shard_map(
        on_device,
        mesh=mesh,
        in_specs=placed,
        out_specs=(
            P("section", None, "shards", "tensor"),
            P("section", None, "shards", "tensor"),
            P("section", "tensor", "shards"),
            P("section", None, "shards", "tensor"),
            P("section", None, "shards", "tensor"),
            P("section", "tensor", "shards"),
            P(("shards", "tensor", "section")),
            P(("shards", "tensor", "section"), None),
            P(("shards", "tensor", "section"), None),
            P(("shards", "tensor", "section"), None),
            P("section", None),
            P("section", None),
            P("section", None),
            P(),
            P(),
            P(),
        ),
        check_vma=False,
    )
```

```python
import math

import jax
import jax.numpy as jnp
from jax import lax
from jax.sharding import PartitionSpec as P

D = 1024
FF = 2816
NS_STEPS = 2


coef_first = 3.4445
coef_second = -4.775
coef_third = 2.0315


def newton_schulz_transposed(rows_bf16):
    as_f32 = rows_bf16.astype(jnp.float32)
    norm_value = jnp.sqrt(jnp.sum(as_f32 * as_f32))
    current = (as_f32 / (norm_value + 1e-07)).astype(jnp.bfloat16)
    for sweep_index in range(NS_STEPS):
        gram_form = lax.dot_general(
            current, current, (((0,), (0,)), ((), ())), preferred_element_type=jnp.float32
        ).astype(jnp.bfloat16)
        square_form = jnp.dot(gram_form, gram_form, preferred_element_type=jnp.float32)
        polynomial = (
            coef_second * gram_form.astype(jnp.float32) + coef_third * square_form
        ).astype(jnp.bfloat16)
        current = (
            coef_first * current.astype(jnp.float32)
            + lax.dot_general(
                current, polynomial, (((1,), (1,)), ((), ())), preferred_element_type=jnp.float32
            )
        ).astype(jnp.bfloat16)
    return current


def refresh(gradient, moment):
    fresh_moment = (0.95 * moment.astype(jnp.float32) + gradient.astype(jnp.float32)).astype(
        jnp.bfloat16
    )
    advance = (gradient.astype(jnp.float32) + 0.95 * fresh_moment.astype(jnp.float32)).astype(
        jnp.bfloat16
    )
    return (fresh_moment, advance)


def adamw_update(weight, gradient, moment, second, decay_rate):
    moment_new = 0.9 * moment + 0.1 * gradient
    second_new = 0.95 * second + 0.05 * gradient * gradient
    weight_new = weight - 0.02 * (moment_new / (jnp.sqrt(second_new) + 1e-08) + decay_rate * weight)
    return (weight_new, moment_new, second_new)


def block_plan(shards_count, tensor_count):
    kind = [0] * (shards_count * tensor_count)
    index = [0] * (shards_count * tensor_count)
    chips = [(x, z) for x in range(shards_count // 2) for z in range(tensor_count)]
    for number, (x, z) in enumerate(chips):
        kind[(2 * x + 1) * tensor_count + z] = 1
        index[(2 * x + 1) * tensor_count + z] = number
    for number, (x, z) in enumerate(chips[:12]):
        kind[(2 * x) * tensor_count + z] = 2
        index[(2 * x) * tensor_count + z] = number
    return kind, index


def on_device(
    attn_grad,
    mlp_in_grad,
    mlp_out_grad,
    attn_momentum,
    mlp_in_momentum,
    mlp_out_momentum,
    owners,
    embed_weight,
    embed_grad,
    embed_moment,
    embed_second,
    norm_scale,
    norm_partial,
    norm_moment,
    norm_second,
    bias_table,
    bias_partial,
    bias_moment,
    bias_second,
):
    shards_count = lax.axis_size("shards")
    tensor_count = lax.axis_size("tensor")
    group_count = shards_count * tensor_count
    my_index = lax.axis_index(("shards", "tensor"))
    my_row = my_index // tensor_count
    my_col = my_index % tensor_count
    layers_here = owners.shape[0]
    rows_block = attn_grad.shape[2]
    cols_block = attn_grad.shape[3]
    ff_block = mlp_in_grad.shape[3]
    square_width = rows_block * cols_block
    rect_width = rows_block * ff_block
    n_square = layers_here * 4
    n_rect = layers_here * 3
    kind_list, index_list = block_plan(shards_count, tensor_count)
    assert sum(k == 1 for k in kind_list) == n_square and sum(k == 2 for k in kind_list) == n_rect
    kind_table = jnp.array(kind_list, jnp.int32)
    index_table = jnp.array(index_list, jnp.int32)
    square_home = [0] * n_square
    rect_home = [0] * n_rect
    for device, (k, i) in enumerate(zip(kind_list, index_list)):
        if k == 1:
            square_home[i] = device
        elif k == 2:
            rect_home[i] = device

    attn_fresh, attn_ahead = refresh(attn_grad, attn_momentum)
    inner_fresh, inner_ahead = refresh(mlp_in_grad, mlp_in_momentum)
    outer_fresh, outer_ahead = refresh(mlp_out_grad, mlp_out_momentum)
    square_table = jnp.swapaxes(attn_ahead, 2, 3).reshape(n_square, cols_block, rows_block)
    rect_table = jnp.concatenate(
        [jnp.swapaxes(inner_ahead, 2, 3), outer_ahead[:, None]], axis=1
    ).reshape(n_rect, ff_block, rows_block)

    square_ss = jnp.sum(jnp.square(square_table.astype(jnp.float32)), axis=(1, 2))
    rect_ss = jnp.sum(jnp.square(rect_table.astype(jnp.float32)), axis=(1, 2))
    def padded(block):
        return jnp.pad(block, ((0, ff_block - block.shape[0]), (0, 0)))

    zero_slot = jnp.zeros((ff_block, rows_block), jnp.bfloat16)
    slots_out = []
    for device in range(group_count):
        if kind_list[device] == 1:
            slots_out.append(padded(square_table[index_list[device]]))
        elif kind_list[device] == 2:
            slots_out.append(rect_table[index_list[device]])
        else:
            slots_out.append(zero_slot)
    outgoing = jnp.stack(slots_out)
    incoming = lax.all_to_all(outgoing, ("shards", "tensor"), split_axis=0, concat_axis=0, tiled=True)

    norm_partial_late, square_ss, rect_ss, bias_partial_late, incoming = lax.optimization_barrier(
        (norm_partial, square_ss, rect_ss, bias_partial, incoming)
    )
    norm_width = norm_partial.shape[0] * norm_partial.shape[2]
    packed = jnp.concatenate([norm_partial_late.reshape(norm_width), square_ss, rect_ss])
    packed = jnp.pad(packed, (0, (-packed.shape[0]) % 128))
    gathered_all = lax.all_gather(packed, ("shards", "tensor"), axis=0, tiled=False)
    bias_flat = bias_partial_late.reshape(-1)
    bias_pad = jnp.pad(bias_flat, (0, 2048 - bias_flat.shape[0]))
    bias_all = lax.all_gather(bias_pad, ("shards", "tensor", "section"), axis=0, tiled=False)

    def run(arrived_blocks, width):
        whole = (
            arrived_blocks[:, :width]
            .reshape(shards_count, tensor_count, width, rows_block)
            .transpose(1, 2, 0, 3)
            .reshape(tensor_count * width, shards_count * rows_block)
        )
        done = newton_schulz_transposed(whole)
        back = (
            done.reshape(tensor_count, width, shards_count, rows_block)
            .transpose(2, 0, 1, 3)
            .reshape(group_count, width, rows_block)
        )
        return jnp.pad(back, ((0, 0), (0, ff_block - width), (0, 0)))

    my_kind = kind_table[my_index]

    def square_branch(arrived_blocks):
        return run(arrived_blocks, cols_block)

    def rect_branch(arrived_blocks):
        return run(arrived_blocks, ff_block)

    def idle_branch(arrived_blocks):
        return jnp.zeros((group_count, ff_block, rows_block), jnp.bfloat16)

    returning = lax.switch(my_kind, [idle_branch, square_branch, rect_branch], incoming)
    returning, gathered_all, bias_all = lax.optimization_barrier((returning, gathered_all, bias_all))
    arrived = lax.all_to_all(returning, ("shards", "tensor"), split_axis=0, concat_axis=0, tiled=True)

    gathered = jnp.sum(gathered_all, axis=0)
    norm_grad = gathered[:norm_width].reshape(norm_partial.shape[0], norm_partial.shape[2])
    square_norm = jnp.sqrt(gathered[norm_width : norm_width + n_square])
    rect_norm = jnp.sqrt(gathered[norm_width + n_square : norm_width + n_square + n_rect])
    bias_grad = jnp.sum(bias_all, axis=0)[: bias_flat.shape[0]].reshape(bias_table.shape)
    rms_all = jnp.concatenate(
        [
            square_norm.reshape(layers_here, 4) / math.sqrt(D * D),
            rect_norm.reshape(layers_here, 3) / math.sqrt(D * FF),
        ],
        axis=1,
    )
    owner_rms = jnp.sum(jnp.where(owners == my_index, rms_all, 0.0)).reshape(1)


    square_rows = jnp.swapaxes(
        jnp.stack([arrived[device, :cols_block] for device in square_home]), 1, 2
    ).reshape(layers_here, 4, rows_block, cols_block).astype(jnp.float32) * (0.2 * math.sqrt(D))
    rect_rows = jnp.stack([arrived[device] for device in rect_home]).reshape(
        layers_here, 3, ff_block, rows_block
    ).astype(jnp.float32) * (0.2 * math.sqrt(FF))
    mlp_in_update = jnp.swapaxes(rect_rows[:, :2], 2, 3)
    mlp_out_update = rect_rows[:, 2]

    embed_results = adamw_update(
        embed_weight, embed_grad.astype(jnp.float32), embed_moment, embed_second, 0.1
    )
    norm_results = adamw_update(norm_scale, norm_grad, norm_moment, norm_second, 0.0)
    bias_results = adamw_update(bias_table, bias_grad, bias_moment, bias_second, 0.0)
    return (
        attn_fresh,
        inner_fresh,
        outer_fresh,
        square_rows,
        mlp_in_update,
        mlp_out_update,
        owner_rms,
        embed_results[0],
        embed_results[1],
        embed_results[2],
        norm_results[0],
        norm_results[1],
        norm_results[2],
        bias_results[0],
        bias_results[1],
        bias_results[2],
    )


def solution(mesh):
    placed = (
        P("section", None, "shards", "tensor"),
        P("section", None, "shards", "tensor"),
        P("section", "tensor", "shards"),
        P("section", None, "shards", "tensor"),
        P("section", None, "shards", "tensor"),
        P("section", "tensor", "shards"),
        P("section", None),
        P(("shards", "tensor", "section"), None),
        P(("shards", "tensor", "section"), None),
        P(("shards", "tensor", "section"), None),
        P(("shards", "tensor", "section"), None),
        P("section", None),
        P("section", ("shards", "tensor"), None),
        P("section", None),
        P("section", None),
        P(),
        P(("shards", "tensor", "section"), None, None),
        P(),
        P(),
    )
    return jax.shard_map(
        on_device,
        mesh=mesh,
        in_specs=placed,
        out_specs=(
            P("section", None, "shards", "tensor"),
            P("section", None, "shards", "tensor"),
            P("section", "tensor", "shards"),
            P("section", None, "shards", "tensor"),
            P("section", None, "shards", "tensor"),
            P("section", "tensor", "shards"),
            P(("shards", "tensor", "section")),
            P(("shards", "tensor", "section"), None),
            P(("shards", "tensor", "section"), None),
            P(("shards", "tensor", "section"), None),
            P("section", None),
            P("section", None),
            P("section", None),
            P(),
            P(),
            P(),
        ),
        check_vma=False,
    )
```

```python
import math

import jax
import jax.numpy as jnp
from jax import lax
from jax.sharding import PartitionSpec as P

D = 1024
FF = 2816
NS_STEPS = 2


coef_first = 3.4445
coef_second = -4.775
coef_third = 2.0315


def newton_schulz_transposed(rows_bf16):
    as_f32 = rows_bf16.astype(jnp.float32)
    norm_value = jnp.sqrt(jnp.sum(as_f32 * as_f32))
    current = (as_f32 / (norm_value + 1e-07)).astype(jnp.bfloat16)
    for sweep_index in range(NS_STEPS):
        gram_form = lax.dot_general(
            current, current, (((0,), (0,)), ((), ())), preferred_element_type=jnp.float32
        ).astype(jnp.bfloat16)
        square_form = jnp.dot(gram_form, gram_form, preferred_element_type=jnp.float32)
        polynomial = (
            coef_second * gram_form.astype(jnp.float32) + coef_third * square_form
        ).astype(jnp.bfloat16)
        current = (
            coef_first * current.astype(jnp.float32)
            + lax.dot_general(
                current, polynomial, (((1,), (1,)), ((), ())), preferred_element_type=jnp.float32
            )
        ).astype(jnp.bfloat16)
    return current


def refresh(gradient, moment):
    fresh_moment = (0.95 * moment.astype(jnp.float32) + gradient.astype(jnp.float32)).astype(
        jnp.bfloat16
    )
    advance = (gradient.astype(jnp.float32) + 0.95 * fresh_moment.astype(jnp.float32)).astype(
        jnp.bfloat16
    )
    return (fresh_moment, advance)


def adamw_update(weight, gradient, moment, second, decay_rate):
    moment_new = 0.9 * moment + 0.1 * gradient
    second_new = 0.95 * second + 0.05 * gradient * gradient
    weight_new = weight - 0.02 * (moment_new / (jnp.sqrt(second_new) + 1e-08) + decay_rate * weight)
    return (weight_new, moment_new, second_new)


def block_plan(shards_count, tensor_count, n_square, n_rect):
    group = shards_count * tensor_count
    kind = [2] * n_rect + [1] * n_square + [0] * (group - n_rect - n_square)
    index = list(range(n_rect)) + list(range(n_square)) + [0] * (group - n_rect - n_square)
    return kind, index


def on_device(
    attn_grad,
    mlp_in_grad,
    mlp_out_grad,
    attn_momentum,
    mlp_in_momentum,
    mlp_out_momentum,
    owners,
    embed_weight,
    embed_grad,
    embed_moment,
    embed_second,
    norm_scale,
    norm_partial,
    norm_moment,
    norm_second,
    bias_table,
    bias_partial,
    bias_moment,
    bias_second,
):
    shards_count = lax.axis_size("shards")
    tensor_count = lax.axis_size("tensor")
    group_count = shards_count * tensor_count
    my_index = lax.axis_index(("shards", "tensor"))
    my_row = my_index // tensor_count
    my_col = my_index % tensor_count
    layers_here = owners.shape[0]
    rows_block = attn_grad.shape[2]
    cols_block = attn_grad.shape[3]
    ff_block = mlp_in_grad.shape[3]
    square_width = rows_block * cols_block
    rect_width = rows_block * ff_block
    n_square = layers_here * 4
    n_rect = layers_here * 3
    kind_list, index_list = block_plan(shards_count, tensor_count, n_square, n_rect)
    assert sum(k == 1 for k in kind_list) == n_square and sum(k == 2 for k in kind_list) == n_rect
    kind_table = jnp.array(kind_list, jnp.int32)
    index_table = jnp.array(index_list, jnp.int32)
    square_home = [0] * n_square
    rect_home = [0] * n_rect
    for device, (k, i) in enumerate(zip(kind_list, index_list)):
        if k == 1:
            square_home[i] = device
        elif k == 2:
            rect_home[i] = device

    attn_fresh, attn_ahead = refresh(attn_grad, attn_momentum)
    inner_fresh, inner_ahead = refresh(mlp_in_grad, mlp_in_momentum)
    outer_fresh, outer_ahead = refresh(mlp_out_grad, mlp_out_momentum)
    square_table = jnp.swapaxes(attn_ahead, 2, 3).reshape(n_square, cols_block, rows_block)
    rect_table = jnp.concatenate(
        [jnp.swapaxes(inner_ahead, 2, 3), outer_ahead[:, None]], axis=1
    ).reshape(n_rect, ff_block, rows_block)

    square_ss = jnp.sum(jnp.square(square_table.astype(jnp.float32)), axis=(1, 2))
    rect_ss = jnp.sum(jnp.square(rect_table.astype(jnp.float32)), axis=(1, 2))
    def padded(block):
        return jnp.pad(block, ((0, ff_block - block.shape[0]), (0, 0)))

    idle_count = group_count - n_rect - n_square
    outgoing = jnp.concatenate(
        [
            rect_table,
            jnp.pad(square_table, ((0, 0), (0, ff_block - cols_block), (0, 0))),
            jnp.zeros((idle_count, ff_block, rows_block), jnp.bfloat16),
        ]
    )
    incoming = lax.all_to_all(outgoing, ("shards", "tensor"), split_axis=0, concat_axis=0, tiled=True)

    norm_partial_late, square_ss, rect_ss, bias_partial_late, incoming = lax.optimization_barrier(
        (norm_partial, square_ss, rect_ss, bias_partial, incoming)
    )
    norm_width = norm_partial.shape[0] * norm_partial.shape[2]
    bias_flat = bias_partial_late.reshape(-1)
    bias_width = bias_flat.shape[0]
    packed = jnp.concatenate([norm_partial_late.reshape(norm_width), bias_flat, square_ss, rect_ss])
    packed = jnp.pad(packed, (0, (-packed.shape[0]) % 128))
    gathered = jnp.sum(lax.all_gather(packed, ("shards", "tensor"), axis=0, tiled=False), axis=0)
    bias_section = jnp.pad(gathered[norm_width : norm_width + bias_width], (0, 65536 - bias_width))
    bias_all = lax.all_gather(bias_section, "section", axis=0, tiled=False)

    def run(arrived_blocks, width):
        whole = (
            arrived_blocks[:, :width]
            .reshape(shards_count, tensor_count, width, rows_block)
            .transpose(1, 2, 0, 3)
            .reshape(tensor_count * width, shards_count * rows_block)
        )
        done = newton_schulz_transposed(whole)
        back = (
            done.reshape(tensor_count, width, shards_count, rows_block)
            .transpose(2, 0, 1, 3)
            .reshape(group_count, width, rows_block)
        )
        return jnp.pad(back, ((0, 0), (0, ff_block - width), (0, 0)))

    my_kind = kind_table[my_index]

    def square_branch(arrived_blocks):
        return run(arrived_blocks, cols_block)

    def rect_branch(arrived_blocks):
        return run(arrived_blocks, ff_block)

    def idle_branch(arrived_blocks):
        return jnp.zeros((group_count, ff_block, rows_block), jnp.bfloat16)

    returning = lax.switch(my_kind, [idle_branch, square_branch, rect_branch], incoming)
    returning, gathered, bias_all = lax.optimization_barrier((returning, gathered, bias_all))
    arrived = lax.all_to_all(returning, ("shards", "tensor"), split_axis=0, concat_axis=0, tiled=True)

    norm_grad = gathered[:norm_width].reshape(norm_partial.shape[0], norm_partial.shape[2])
    ss_start = norm_width + bias_width
    square_norm = jnp.sqrt(gathered[ss_start : ss_start + n_square])
    rect_norm = jnp.sqrt(gathered[ss_start + n_square : ss_start + n_square + n_rect])
    bias_grad = jnp.sum(bias_all, axis=0)[:bias_width].reshape(bias_table.shape)
    rms_all = jnp.concatenate(
        [
            square_norm.reshape(layers_here, 4) / math.sqrt(D * D),
            rect_norm.reshape(layers_here, 3) / math.sqrt(D * FF),
        ],
        axis=1,
    )
    owner_rms = jnp.sum(jnp.where(owners == my_index, rms_all, 0.0)).reshape(1)


    square_rows = jnp.swapaxes(
        jnp.stack([arrived[device, :cols_block] for device in square_home]), 1, 2
    ).reshape(layers_here, 4, rows_block, cols_block).astype(jnp.float32) * (0.2 * math.sqrt(D))
    rect_rows = jnp.stack([arrived[device] for device in rect_home]).reshape(
        layers_here, 3, ff_block, rows_block
    ).astype(jnp.float32) * (0.2 * math.sqrt(FF))
    mlp_in_update = jnp.swapaxes(rect_rows[:, :2], 2, 3)
    mlp_out_update = rect_rows[:, 2]

    embed_results = adamw_update(
        embed_weight, embed_grad.astype(jnp.float32), embed_moment, embed_second, 0.1
    )
    norm_results = adamw_update(norm_scale, norm_grad, norm_moment, norm_second, 0.0)
    bias_results = adamw_update(bias_table, bias_grad, bias_moment, bias_second, 0.0)
    return (
        attn_fresh,
        inner_fresh,
        outer_fresh,
        square_rows,
        mlp_in_update,
        mlp_out_update,
        owner_rms,
        embed_results[0],
        embed_results[1],
        embed_results[2],
        norm_results[0],
        norm_results[1],
        norm_results[2],
        bias_results[0],
        bias_results[1],
        bias_results[2],
    )


def solution(mesh):
    placed = (
        P("section", None, "shards", "tensor"),
        P("section", None, "shards", "tensor"),
        P("section", "tensor", "shards"),
        P("section", None, "shards", "tensor"),
        P("section", None, "shards", "tensor"),
        P("section", "tensor", "shards"),
        P("section", None),
        P(("shards", "tensor", "section"), None),
        P(("shards", "tensor", "section"), None),
        P(("shards", "tensor", "section"), None),
        P(("shards", "tensor", "section"), None),
        P("section", None),
        P("section", ("shards", "tensor"), None),
        P("section", None),
        P("section", None),
        P(),
        P(("shards", "tensor", "section"), None, None),
        P(),
        P(),
    )
    return jax.shard_map(
        on_device,
        mesh=mesh,
        in_specs=placed,
        out_specs=(
            P("section", None, "shards", "tensor"),
            P("section", None, "shards", "tensor"),
            P("section", "tensor", "shards"),
            P("section", None, "shards", "tensor"),
            P("section", None, "shards", "tensor"),
            P("section", "tensor", "shards"),
            P(("shards", "tensor", "section")),
            P(("shards", "tensor", "section"), None),
            P(("shards", "tensor", "section"), None),
            P(("shards", "tensor", "section"), None),
            P("section", None),
            P("section", None),
            P("section", None),
            P(),
            P(),
            P(),
        ),
        check_vma=False,
    )
```

```python
import math

import jax
import jax.numpy as jnp
from jax import lax
from jax.sharding import PartitionSpec as P

D = 1024
FF = 2816
NS_STEPS = 2


coef_first = 3.4445
coef_second = -4.775
coef_third = 2.0315


def newton_schulz_transposed(rows_bf16):
    as_f32 = rows_bf16.astype(jnp.float32)
    norm_value = jnp.sqrt(jnp.sum(as_f32 * as_f32))
    current = (as_f32 / (norm_value + 1e-07)).astype(jnp.bfloat16)
    for sweep_index in range(NS_STEPS):
        gram_form = lax.dot_general(
            current, current, (((0,), (0,)), ((), ())), preferred_element_type=jnp.float32
        ).astype(jnp.bfloat16)
        square_form = jnp.dot(gram_form, gram_form, preferred_element_type=jnp.float32)
        polynomial = (
            coef_second * gram_form.astype(jnp.float32) + coef_third * square_form
        ).astype(jnp.bfloat16)
        current = (
            coef_first * current.astype(jnp.float32)
            + lax.dot_general(
                current, polynomial, (((1,), (1,)), ((), ())), preferred_element_type=jnp.float32
            )
        ).astype(jnp.bfloat16)
    return current


def refresh(gradient, moment):
    fresh_moment = (0.95 * moment.astype(jnp.float32) + gradient.astype(jnp.float32)).astype(
        jnp.bfloat16
    )
    advance = (gradient.astype(jnp.float32) + 0.95 * fresh_moment.astype(jnp.float32)).astype(
        jnp.bfloat16
    )
    return (fresh_moment, advance)


def adamw_update(weight, gradient, moment, second, decay_rate):
    moment_new = 0.9 * moment + 0.1 * gradient
    second_new = 0.95 * second + 0.05 * gradient * gradient
    weight_new = weight - 0.02 * (moment_new / (jnp.sqrt(second_new) + 1e-08) + decay_rate * weight)
    return (weight_new, moment_new, second_new)


def block_plan(shards_count, tensor_count, n_square, n_rect):
    group = shards_count * tensor_count
    kind = [2] * n_rect + [1] * n_square + [0] * (group - n_rect - n_square)
    index = list(range(n_rect)) + list(range(n_square)) + [0] * (group - n_rect - n_square)
    return kind, index


def on_device(
    attn_grad,
    mlp_in_grad,
    mlp_out_grad,
    attn_momentum,
    mlp_in_momentum,
    mlp_out_momentum,
    owners,
    embed_weight,
    embed_grad,
    embed_moment,
    embed_second,
    norm_scale,
    norm_partial,
    norm_moment,
    norm_second,
    bias_table,
    bias_partial,
    bias_moment,
    bias_second,
):
    shards_count = lax.axis_size("shards")
    tensor_count = lax.axis_size("tensor")
    group_count = shards_count * tensor_count
    my_index = lax.axis_index(("shards", "tensor"))
    my_row = my_index // tensor_count
    my_col = my_index % tensor_count
    layers_here = owners.shape[0]
    rows_block = attn_grad.shape[2]
    cols_block = attn_grad.shape[3]
    ff_block = mlp_in_grad.shape[3]
    square_width = rows_block * cols_block
    rect_width = rows_block * ff_block
    n_square = layers_here * 4
    n_rect = layers_here * 3
    kind_list, index_list = block_plan(shards_count, tensor_count, n_square, n_rect)
    assert sum(k == 1 for k in kind_list) == n_square and sum(k == 2 for k in kind_list) == n_rect
    kind_table = jnp.array(kind_list, jnp.int32)
    index_table = jnp.array(index_list, jnp.int32)
    square_home = [0] * n_square
    rect_home = [0] * n_rect
    for device, (k, i) in enumerate(zip(kind_list, index_list)):
        if k == 1:
            square_home[i] = device
        elif k == 2:
            rect_home[i] = device

    attn_fresh, attn_ahead = refresh(attn_grad, attn_momentum)
    inner_fresh, inner_ahead = refresh(mlp_in_grad, mlp_in_momentum)
    outer_fresh, outer_ahead = refresh(mlp_out_grad, mlp_out_momentum)
    square_table = jnp.swapaxes(attn_ahead, 2, 3).reshape(n_square, cols_block, rows_block)
    rect_table = jnp.concatenate(
        [jnp.swapaxes(inner_ahead, 2, 3), outer_ahead[:, None]], axis=1
    ).reshape(n_rect, ff_block, rows_block)

    square_ss = jnp.sum(jnp.square(square_table.astype(jnp.float32)), axis=(1, 2))
    rect_ss = jnp.sum(jnp.square(rect_table.astype(jnp.float32)), axis=(1, 2))
    def padded(block):
        return jnp.pad(block, ((0, ff_block - block.shape[0]), (0, 0)))

    bias_flat = bias_partial.reshape(-1)
    bias_across = lax.all_gather(
        jnp.pad(bias_flat, (0, 65536 - bias_flat.shape[0])), "section", axis=0, tiled=False
    )
    bias_sections = jnp.sum(bias_across[:, : bias_flat.shape[0]], axis=0)

    idle_count = group_count - n_rect - n_square
    outgoing = jnp.concatenate(
        [
            rect_table,
            jnp.pad(square_table, ((0, 0), (0, ff_block - cols_block), (0, 0))),
            jnp.zeros((idle_count, ff_block, rows_block), jnp.bfloat16),
        ]
    )
    incoming = lax.all_to_all(outgoing, ("shards", "tensor"), split_axis=0, concat_axis=0, tiled=True)

    norm_partial_late, square_ss, rect_ss, bias_sections, incoming = lax.optimization_barrier(
        (norm_partial, square_ss, rect_ss, bias_sections, incoming)
    )
    norm_width = norm_partial.shape[0] * norm_partial.shape[2]
    bias_width = bias_sections.shape[0]
    packed = jnp.concatenate([norm_partial_late.reshape(norm_width), bias_sections, square_ss, rect_ss])
    packed = jnp.pad(packed, (0, (-packed.shape[0]) % 128))
    gathered = jnp.sum(lax.all_gather(packed, ("shards", "tensor"), axis=0, tiled=False), axis=0)

    def run(arrived_blocks, width):
        whole = (
            arrived_blocks[:, :width]
            .reshape(shards_count, tensor_count, width, rows_block)
            .transpose(1, 2, 0, 3)
            .reshape(tensor_count * width, shards_count * rows_block)
        )
        done = newton_schulz_transposed(whole)
        back = (
            done.reshape(tensor_count, width, shards_count, rows_block)
            .transpose(2, 0, 1, 3)
            .reshape(group_count, width, rows_block)
        )
        return jnp.pad(back, ((0, 0), (0, ff_block - width), (0, 0)))

    my_kind = kind_table[my_index]

    def square_branch(arrived_blocks):
        return run(arrived_blocks, cols_block)

    def rect_branch(arrived_blocks):
        return run(arrived_blocks, ff_block)

    def idle_branch(arrived_blocks):
        return jnp.zeros((group_count, ff_block, rows_block), jnp.bfloat16)

    returning = lax.switch(my_kind, [idle_branch, square_branch, rect_branch], incoming)
    returning, gathered = lax.optimization_barrier((returning, gathered))
    arrived = lax.all_to_all(returning, ("shards", "tensor"), split_axis=0, concat_axis=0, tiled=True)

    norm_grad = gathered[:norm_width].reshape(norm_partial.shape[0], norm_partial.shape[2])
    ss_start = norm_width + bias_width
    square_norm = jnp.sqrt(gathered[ss_start : ss_start + n_square])
    rect_norm = jnp.sqrt(gathered[ss_start + n_square : ss_start + n_square + n_rect])
    bias_grad = gathered[norm_width : norm_width + bias_width].reshape(bias_table.shape)
    rms_all = jnp.concatenate(
        [
            square_norm.reshape(layers_here, 4) / math.sqrt(D * D),
            rect_norm.reshape(layers_here, 3) / math.sqrt(D * FF),
        ],
        axis=1,
    )
    owner_rms = jnp.sum(jnp.where(owners == my_index, rms_all, 0.0)).reshape(1)


    square_rows = jnp.swapaxes(
        jnp.stack([arrived[device, :cols_block] for device in square_home]), 1, 2
    ).reshape(layers_here, 4, rows_block, cols_block).astype(jnp.float32) * (0.2 * math.sqrt(D))
    rect_rows = jnp.stack([arrived[device] for device in rect_home]).reshape(
        layers_here, 3, ff_block, rows_block
    ).astype(jnp.float32) * (0.2 * math.sqrt(FF))
    mlp_in_update = jnp.swapaxes(rect_rows[:, :2], 2, 3)
    mlp_out_update = rect_rows[:, 2]

    embed_results = adamw_update(
        embed_weight, embed_grad.astype(jnp.float32), embed_moment, embed_second, 0.1
    )
    norm_results = adamw_update(norm_scale, norm_grad, norm_moment, norm_second, 0.0)
    bias_results = adamw_update(bias_table, bias_grad, bias_moment, bias_second, 0.0)
    return (
        attn_fresh,
        inner_fresh,
        outer_fresh,
        square_rows,
        mlp_in_update,
        mlp_out_update,
        owner_rms,
        embed_results[0],
        embed_results[1],
        embed_results[2],
        norm_results[0],
        norm_results[1],
        norm_results[2],
        bias_results[0],
        bias_results[1],
        bias_results[2],
    )


def solution(mesh):
    placed = (
        P("section", None, "shards", "tensor"),
        P("section", None, "shards", "tensor"),
        P("section", "tensor", "shards"),
        P("section", None, "shards", "tensor"),
        P("section", None, "shards", "tensor"),
        P("section", "tensor", "shards"),
        P("section", None),
        P(("shards", "tensor", "section"), None),
        P(("shards", "tensor", "section"), None),
        P(("shards", "tensor", "section"), None),
        P(("shards", "tensor", "section"), None),
        P("section", None),
        P("section", ("shards", "tensor"), None),
        P("section", None),
        P("section", None),
        P(),
        P(("shards", "tensor", "section"), None, None),
        P(),
        P(),
    )
    return jax.shard_map(
        on_device,
        mesh=mesh,
        in_specs=placed,
        out_specs=(
            P("section", None, "shards", "tensor"),
            P("section", None, "shards", "tensor"),
            P("section", "tensor", "shards"),
            P("section", None, "shards", "tensor"),
            P("section", None, "shards", "tensor"),
            P("section", "tensor", "shards"),
            P(("shards", "tensor", "section")),
            P(("shards", "tensor", "section"), None),
            P(("shards", "tensor", "section"), None),
            P(("shards", "tensor", "section"), None),
            P("section", None),
            P("section", None),
            P("section", None),
            P(),
            P(),
            P(),
        ),
        check_vma=False,
    )
```

```python
import math

import jax
import jax.numpy as jnp
from jax import lax
from jax.sharding import PartitionSpec as P

D = 1024
FF = 2816
NS_STEPS = 2


coef_first = 3.4445
coef_second = -4.775
coef_third = 2.0315


def newton_schulz_transposed(rows_bf16, norm_value):
    current = (rows_bf16.astype(jnp.float32) / (norm_value + 1e-07)).astype(jnp.bfloat16)
    for sweep_index in range(NS_STEPS):
        gram_form = lax.dot_general(
            current, current, (((0,), (0,)), ((), ())), preferred_element_type=jnp.float32
        ).astype(jnp.bfloat16)
        square_form = jnp.dot(gram_form, gram_form, preferred_element_type=jnp.float32)
        polynomial = (
            coef_second * gram_form.astype(jnp.float32) + coef_third * square_form
        ).astype(jnp.bfloat16)
        current = (
            coef_first * current.astype(jnp.float32)
            + lax.dot_general(
                current, polynomial, (((1,), (1,)), ((), ())), preferred_element_type=jnp.float32
            )
        ).astype(jnp.bfloat16)
    return current


def refresh(gradient, moment):
    fresh_moment = (0.95 * moment.astype(jnp.float32) + gradient.astype(jnp.float32)).astype(
        jnp.bfloat16
    )
    advance = (gradient.astype(jnp.float32) + 0.95 * fresh_moment.astype(jnp.float32)).astype(
        jnp.bfloat16
    )
    return (fresh_moment, advance)


def adamw_update(weight, gradient, moment, second, decay_rate):
    moment_new = 0.9 * moment + 0.1 * gradient
    second_new = 0.95 * second + 0.05 * gradient * gradient
    weight_new = weight - 0.02 * (moment_new / (jnp.sqrt(second_new) + 1e-08) + decay_rate * weight)
    return (weight_new, moment_new, second_new)


def block_plan(shards_count, tensor_count, n_square, n_rect):
    group = shards_count * tensor_count
    kind = [2] * n_rect + [1] * n_square + [0] * (group - n_rect - n_square)
    index = list(range(n_rect)) + list(range(n_square)) + [0] * (group - n_rect - n_square)
    return kind, index


def on_device(
    attn_grad,
    mlp_in_grad,
    mlp_out_grad,
    attn_momentum,
    mlp_in_momentum,
    mlp_out_momentum,
    owners,
    embed_weight,
    embed_grad,
    embed_moment,
    embed_second,
    norm_scale,
    norm_partial,
    norm_moment,
    norm_second,
    bias_table,
    bias_partial,
    bias_moment,
    bias_second,
):
    shards_count = lax.axis_size("shards")
    tensor_count = lax.axis_size("tensor")
    group_count = shards_count * tensor_count
    my_index = lax.axis_index(("shards", "tensor"))
    my_row = my_index // tensor_count
    my_col = my_index % tensor_count
    layers_here = owners.shape[0]
    rows_block = attn_grad.shape[2]
    cols_block = attn_grad.shape[3]
    ff_block = mlp_in_grad.shape[3]
    square_width = rows_block * cols_block
    rect_width = rows_block * ff_block
    n_square = layers_here * 4
    n_rect = layers_here * 3
    kind_list, index_list = block_plan(shards_count, tensor_count, n_square, n_rect)
    assert sum(k == 1 for k in kind_list) == n_square and sum(k == 2 for k in kind_list) == n_rect
    kind_table = jnp.array(kind_list, jnp.int32)
    index_table = jnp.array(index_list, jnp.int32)
    square_home = [0] * n_square
    rect_home = [0] * n_rect
    for device, (k, i) in enumerate(zip(kind_list, index_list)):
        if k == 1:
            square_home[i] = device
        elif k == 2:
            rect_home[i] = device

    attn_fresh, attn_ahead = refresh(attn_grad, attn_momentum)
    inner_fresh, inner_ahead = refresh(mlp_in_grad, mlp_in_momentum)
    outer_fresh, outer_ahead = refresh(mlp_out_grad, mlp_out_momentum)
    square_table = jnp.swapaxes(attn_ahead, 2, 3).reshape(n_square, cols_block, rows_block)
    rect_table = jnp.concatenate(
        [jnp.swapaxes(inner_ahead, 2, 3), outer_ahead[:, None]], axis=1
    ).reshape(n_rect, ff_block, rows_block)

    square_ss = jnp.sum(jnp.square(square_table.astype(jnp.float32)), axis=(1, 2))
    rect_ss = jnp.sum(jnp.square(rect_table.astype(jnp.float32)), axis=(1, 2))
    def padded(block):
        return jnp.pad(block, ((0, ff_block - block.shape[0]), (0, 0)))

    norm_width = norm_partial.shape[0] * norm_partial.shape[2]
    bias_flat = bias_partial.reshape(-1)
    bias_width = bias_flat.shape[0]
    packed = jnp.concatenate([norm_partial.reshape(norm_width), bias_flat, square_ss, rect_ss])
    packed = jnp.pad(packed, (0, (-packed.shape[0]) % 128))
    gathered = jnp.sum(lax.all_gather(packed, ("shards", "tensor"), axis=0, tiled=False), axis=0)
    ss_start = norm_width + bias_width
    square_norm = jnp.sqrt(gathered[ss_start : ss_start + n_square])
    rect_norm = jnp.sqrt(gathered[ss_start + n_square : ss_start + n_square + n_rect])

    idle_count = group_count - n_rect - n_square
    outgoing = jnp.concatenate(
        [
            rect_table,
            jnp.pad(square_table, ((0, 0), (0, ff_block - cols_block), (0, 0))),
            jnp.zeros((idle_count, ff_block, rows_block), jnp.bfloat16),
        ]
    )
    incoming = lax.all_to_all(outgoing, ("shards", "tensor"), split_axis=0, concat_axis=0, tiled=True)

    bias_group, incoming = lax.optimization_barrier(
        (gathered[norm_width : norm_width + bias_width], incoming)
    )
    bias_all = lax.all_gather(
        jnp.pad(bias_group, (0, 65536 - bias_width)), "section", axis=0, tiled=False
    )

    def run(arrived_blocks, width, norm_value):
        whole = (
            arrived_blocks[:, :width]
            .reshape(shards_count, tensor_count, width, rows_block)
            .transpose(1, 2, 0, 3)
            .reshape(tensor_count * width, shards_count * rows_block)
        )
        done = newton_schulz_transposed(whole, norm_value)
        back = (
            done.reshape(tensor_count, width, shards_count, rows_block)
            .transpose(2, 0, 1, 3)
            .reshape(group_count, width, rows_block)
        )
        return jnp.pad(back, ((0, 0), (0, ff_block - width), (0, 0)))

    my_kind = kind_table[my_index]
    my_mat = index_table[my_index]

    def square_branch(arrived_blocks):
        return run(arrived_blocks, cols_block, square_norm[my_mat])

    def rect_branch(arrived_blocks):
        return run(arrived_blocks, ff_block, rect_norm[my_mat])

    def idle_branch(arrived_blocks):
        return jnp.zeros((group_count, ff_block, rows_block), jnp.bfloat16)

    returning = lax.switch(my_kind, [idle_branch, square_branch, rect_branch], incoming)
    returning, bias_all = lax.optimization_barrier((returning, bias_all))
    arrived = lax.all_to_all(returning, ("shards", "tensor"), split_axis=0, concat_axis=0, tiled=True)

    norm_grad = gathered[:norm_width].reshape(norm_partial.shape[0], norm_partial.shape[2])
    bias_grad = jnp.sum(bias_all[:, :bias_width], axis=0).reshape(bias_table.shape)
    rms_all = jnp.concatenate(
        [
            square_norm.reshape(layers_here, 4) / math.sqrt(D * D),
            rect_norm.reshape(layers_here, 3) / math.sqrt(D * FF),
        ],
        axis=1,
    )
    owner_rms = jnp.sum(jnp.where(owners == my_index, rms_all, 0.0)).reshape(1)


    square_rows = jnp.swapaxes(
        jnp.stack([arrived[device, :cols_block] for device in square_home]), 1, 2
    ).reshape(layers_here, 4, rows_block, cols_block).astype(jnp.float32) * (0.2 * math.sqrt(D))
    rect_rows = jnp.stack([arrived[device] for device in rect_home]).reshape(
        layers_here, 3, ff_block, rows_block
    ).astype(jnp.float32) * (0.2 * math.sqrt(FF))
    mlp_in_update = jnp.swapaxes(rect_rows[:, :2], 2, 3)
    mlp_out_update = rect_rows[:, 2]

    embed_results = adamw_update(
        embed_weight, embed_grad.astype(jnp.float32), embed_moment, embed_second, 0.1
    )
    norm_results = adamw_update(norm_scale, norm_grad, norm_moment, norm_second, 0.0)
    bias_results = adamw_update(bias_table, bias_grad, bias_moment, bias_second, 0.0)
    return (
        attn_fresh,
        inner_fresh,
        outer_fresh,
        square_rows,
        mlp_in_update,
        mlp_out_update,
        owner_rms,
        embed_results[0],
        embed_results[1],
        embed_results[2],
        norm_results[0],
        norm_results[1],
        norm_results[2],
        bias_results[0],
        bias_results[1],
        bias_results[2],
    )


def solution(mesh):
    placed = (
        P("section", None, "shards", "tensor"),
        P("section", None, "shards", "tensor"),
        P("section", "tensor", "shards"),
        P("section", None, "shards", "tensor"),
        P("section", None, "shards", "tensor"),
        P("section", "tensor", "shards"),
        P("section", None),
        P(("shards", "tensor", "section"), None),
        P(("shards", "tensor", "section"), None),
        P(("shards", "tensor", "section"), None),
        P(("shards", "tensor", "section"), None),
        P("section", None),
        P("section", ("shards", "tensor"), None),
        P("section", None),
        P("section", None),
        P(),
        P(("shards", "tensor", "section"), None, None),
        P(),
        P(),
    )
    return jax.shard_map(
        on_device,
        mesh=mesh,
        in_specs=placed,
        out_specs=(
            P("section", None, "shards", "tensor"),
            P("section", None, "shards", "tensor"),
            P("section", "tensor", "shards"),
            P("section", None, "shards", "tensor"),
            P("section", None, "shards", "tensor"),
            P("section", "tensor", "shards"),
            P(("shards", "tensor", "section")),
            P(("shards", "tensor", "section"), None),
            P(("shards", "tensor", "section"), None),
            P(("shards", "tensor", "section"), None),
            P("section", None),
            P("section", None),
            P("section", None),
            P(),
            P(),
            P(),
        ),
        check_vma=False,
    )
```

```python
import math

import jax
import jax.numpy as jnp
from jax import lax
from jax.sharding import PartitionSpec as P

D = 1024
FF = 2816
NS_STEPS = 2


coef_first = 3.4445
coef_second = -4.775
coef_third = 2.0315


def newton_schulz_transposed(rows_bf16):
    as_f32 = rows_bf16.astype(jnp.float32)
    norm_value = jnp.sqrt(jnp.sum(as_f32 * as_f32))
    current = (as_f32 / (norm_value + 1e-07)).astype(jnp.bfloat16)
    for sweep_index in range(NS_STEPS):
        gram_form = lax.dot_general(
            current, current, (((0,), (0,)), ((), ())), preferred_element_type=jnp.float32
        ).astype(jnp.bfloat16)
        square_form = jnp.dot(gram_form, gram_form, preferred_element_type=jnp.float32)
        polynomial = (
            coef_second * gram_form.astype(jnp.float32) + coef_third * square_form
        ).astype(jnp.bfloat16)
        current = (
            coef_first * current.astype(jnp.float32)
            + lax.dot_general(
                current, polynomial, (((1,), (1,)), ((), ())), preferred_element_type=jnp.float32
            )
        ).astype(jnp.bfloat16)
    return current


def refresh(gradient, moment):
    fresh_moment = (0.95 * moment.astype(jnp.float32) + gradient.astype(jnp.float32)).astype(
        jnp.bfloat16
    )
    advance = (gradient.astype(jnp.float32) + 0.95 * fresh_moment.astype(jnp.float32)).astype(
        jnp.bfloat16
    )
    return (fresh_moment, advance)


def adamw_update(weight, gradient, moment, second, decay_rate):
    moment_new = 0.9 * moment + 0.1 * gradient
    second_new = 0.95 * second + 0.05 * gradient * gradient
    weight_new = weight - 0.02 * (moment_new / (jnp.sqrt(second_new) + 1e-08) + decay_rate * weight)
    return (weight_new, moment_new, second_new)


def block_plan(shards_count, tensor_count, n_square, n_rect):
    group = shards_count * tensor_count
    kind = [2] * n_rect + [1] * n_square + [0] * (group - n_rect - n_square)
    index = list(range(n_rect)) + list(range(n_square)) + [0] * (group - n_rect - n_square)
    return kind, index


def on_device(
    attn_grad,
    mlp_in_grad,
    mlp_out_grad,
    attn_momentum,
    mlp_in_momentum,
    mlp_out_momentum,
    owners,
    embed_weight,
    embed_grad,
    embed_moment,
    embed_second,
    norm_scale,
    norm_partial,
    norm_moment,
    norm_second,
    bias_table,
    bias_partial,
    bias_moment,
    bias_second,
):
    shards_count = lax.axis_size("shards")
    tensor_count = lax.axis_size("tensor")
    group_count = shards_count * tensor_count
    my_index = lax.axis_index(("shards", "tensor"))
    my_row = my_index // tensor_count
    my_col = my_index % tensor_count
    layers_here = owners.shape[0]
    rows_block = attn_grad.shape[2]
    cols_block = attn_grad.shape[3]
    ff_block = mlp_in_grad.shape[3]
    square_width = rows_block * cols_block
    rect_width = rows_block * ff_block
    n_square = layers_here * 4
    n_rect = layers_here * 3
    kind_list, index_list = block_plan(shards_count, tensor_count, n_square, n_rect)
    assert sum(k == 1 for k in kind_list) == n_square and sum(k == 2 for k in kind_list) == n_rect
    square_home = [0] * n_square
    rect_home = [0] * n_rect
    for device, (k, i) in enumerate(zip(kind_list, index_list)):
        if k == 1:
            square_home[i] = device
        elif k == 2:
            rect_home[i] = device

    attn_fresh, attn_ahead = refresh(attn_grad, attn_momentum)
    inner_fresh, inner_ahead = refresh(mlp_in_grad, mlp_in_momentum)
    outer_fresh, outer_ahead = refresh(mlp_out_grad, mlp_out_momentum)
    square_table = jnp.swapaxes(attn_ahead, 2, 3).reshape(n_square, cols_block, rows_block)
    rect_table = jnp.concatenate(
        [jnp.swapaxes(inner_ahead, 2, 3), outer_ahead[:, None]], axis=1
    ).reshape(n_rect, ff_block, rows_block)

    square_ss = jnp.sum(jnp.square(square_table.astype(jnp.float32)), axis=(1, 2))
    rect_ss = jnp.sum(jnp.square(rect_table.astype(jnp.float32)), axis=(1, 2))
    def padded(block):
        return jnp.pad(block, ((0, ff_block - block.shape[0]), (0, 0)))

    bias_flat = bias_partial.reshape(-1)
    bias_across = lax.all_gather(
        jnp.pad(bias_flat, (0, 65536 - bias_flat.shape[0])), "section", axis=0, tiled=False
    )
    bias_sections = jnp.sum(bias_across[:, : bias_flat.shape[0]], axis=0)

    idle_count = group_count - n_rect - n_square
    outgoing = jnp.concatenate(
        [
            rect_table,
            jnp.pad(square_table, ((0, 0), (0, ff_block - cols_block), (0, 0))),
            jnp.zeros((idle_count, ff_block, rows_block), jnp.bfloat16),
        ]
    )
    incoming = lax.all_to_all(outgoing, ("shards", "tensor"), split_axis=0, concat_axis=0, tiled=True)

    norm_partial_late, square_ss, rect_ss, bias_sections, incoming = lax.optimization_barrier(
        (norm_partial, square_ss, rect_ss, bias_sections, incoming)
    )
    norm_width = norm_partial.shape[0] * norm_partial.shape[2]
    bias_width = bias_sections.shape[0]
    packed = jnp.concatenate([norm_partial_late.reshape(norm_width), bias_sections, square_ss, rect_ss])
    packed = jnp.pad(packed, (0, (-packed.shape[0]) % 128))
    gathered = jnp.sum(lax.all_gather(packed, ("shards", "tensor"), axis=0, tiled=False), axis=0)

    def run(arrived_blocks, width):
        whole = (
            arrived_blocks[:, :width]
            .reshape(shards_count, tensor_count, width, rows_block)
            .transpose(1, 2, 0, 3)
            .reshape(tensor_count * width, shards_count * rows_block)
        )
        done = newton_schulz_transposed(whole)
        back = (
            done.reshape(tensor_count, width, shards_count, rows_block)
            .transpose(2, 0, 1, 3)
            .reshape(group_count, width, rows_block)
        )
        return jnp.pad(back, ((0, 0), (0, ff_block - width), (0, 0)))

    returning = run(incoming, ff_block)
    returning, gathered = lax.optimization_barrier((returning, gathered))
    arrived = lax.all_to_all(returning, ("shards", "tensor"), split_axis=0, concat_axis=0, tiled=True)

    norm_grad = gathered[:norm_width].reshape(norm_partial.shape[0], norm_partial.shape[2])
    ss_start = norm_width + bias_width
    square_norm = jnp.sqrt(gathered[ss_start : ss_start + n_square])
    rect_norm = jnp.sqrt(gathered[ss_start + n_square : ss_start + n_square + n_rect])
    bias_grad = gathered[norm_width : norm_width + bias_width].reshape(bias_table.shape)
    rms_all = jnp.concatenate(
        [
            square_norm.reshape(layers_here, 4) / math.sqrt(D * D),
            rect_norm.reshape(layers_here, 3) / math.sqrt(D * FF),
        ],
        axis=1,
    )
    owner_rms = jnp.sum(jnp.where(owners == my_index, rms_all, 0.0)).reshape(1)


    square_rows = jnp.swapaxes(
        jnp.stack([arrived[device, :cols_block] for device in square_home]), 1, 2
    ).reshape(layers_here, 4, rows_block, cols_block).astype(jnp.float32) * (0.2 * math.sqrt(D))
    rect_rows = jnp.stack([arrived[device] for device in rect_home]).reshape(
        layers_here, 3, ff_block, rows_block
    ).astype(jnp.float32) * (0.2 * math.sqrt(FF))
    mlp_in_update = jnp.swapaxes(rect_rows[:, :2], 2, 3)
    mlp_out_update = rect_rows[:, 2]

    embed_results = adamw_update(
        embed_weight, embed_grad.astype(jnp.float32), embed_moment, embed_second, 0.1
    )
    norm_results = adamw_update(norm_scale, norm_grad, norm_moment, norm_second, 0.0)
    bias_results = adamw_update(bias_table, bias_grad, bias_moment, bias_second, 0.0)
    return (
        attn_fresh,
        inner_fresh,
        outer_fresh,
        square_rows,
        mlp_in_update,
        mlp_out_update,
        owner_rms,
        embed_results[0],
        embed_results[1],
        embed_results[2],
        norm_results[0],
        norm_results[1],
        norm_results[2],
        bias_results[0],
        bias_results[1],
        bias_results[2],
    )


def solution(mesh):
    placed = (
        P("section", None, "shards", "tensor"),
        P("section", None, "shards", "tensor"),
        P("section", "tensor", "shards"),
        P("section", None, "shards", "tensor"),
        P("section", None, "shards", "tensor"),
        P("section", "tensor", "shards"),
        P("section", None),
        P(("shards", "tensor", "section"), None),
        P(("shards", "tensor", "section"), None),
        P(("shards", "tensor", "section"), None),
        P(("shards", "tensor", "section"), None),
        P("section", None),
        P("section", ("shards", "tensor"), None),
        P("section", None),
        P("section", None),
        P(),
        P(("shards", "tensor", "section"), None, None),
        P(),
        P(),
    )
    return jax.shard_map(
        on_device,
        mesh=mesh,
        in_specs=placed,
        out_specs=(
            P("section", None, "shards", "tensor"),
            P("section", None, "shards", "tensor"),
            P("section", "tensor", "shards"),
            P("section", None, "shards", "tensor"),
            P("section", None, "shards", "tensor"),
            P("section", "tensor", "shards"),
            P(("shards", "tensor", "section")),
            P(("shards", "tensor", "section"), None),
            P(("shards", "tensor", "section"), None),
            P(("shards", "tensor", "section"), None),
            P("section", None),
            P("section", None),
            P("section", None),
            P(),
            P(),
            P(),
        ),
        check_vma=False,
    )
```

```python
import math

import jax
import jax.numpy as jnp
from jax import lax
from jax.sharding import PartitionSpec as P

D = 1024
FF = 2816
NS_STEPS = 2


coef_first = 3.4445
coef_second = -4.775
coef_third = 2.0315


def newton_schulz_transposed(rows_bf16):
    as_f32 = rows_bf16.astype(jnp.float32)
    norm_value = jnp.sqrt(jnp.sum(as_f32 * as_f32))
    current = (as_f32 / (norm_value + 1e-07)).astype(jnp.bfloat16)
    for sweep_index in range(NS_STEPS):
        gram_form = lax.dot_general(
            current, current, (((0,), (0,)), ((), ())), preferred_element_type=jnp.float32
        ).astype(jnp.bfloat16)
        square_form = jnp.dot(gram_form, gram_form, preferred_element_type=jnp.float32)
        polynomial = (
            coef_second * gram_form.astype(jnp.float32) + coef_third * square_form
        ).astype(jnp.bfloat16)
        current = (
            coef_first * current.astype(jnp.float32)
            + lax.dot_general(
                current, polynomial, (((1,), (1,)), ((), ())), preferred_element_type=jnp.float32
            )
        ).astype(jnp.bfloat16)
    return current


def refresh(gradient, moment):
    fresh_moment = (0.95 * moment.astype(jnp.float32) + gradient.astype(jnp.float32)).astype(
        jnp.bfloat16
    )
    advance = (gradient.astype(jnp.float32) + 0.95 * fresh_moment.astype(jnp.float32)).astype(
        jnp.bfloat16
    )
    return (fresh_moment, advance)


def adamw_update(weight, gradient, moment, second, decay_rate):
    moment_new = 0.9 * moment + 0.1 * gradient
    second_new = 0.95 * second + 0.05 * gradient * gradient
    weight_new = weight - 0.02 * (moment_new / (jnp.sqrt(second_new) + 1e-08) + decay_rate * weight)
    return (weight_new, moment_new, second_new)


def block_plan(shards_count, tensor_count, n_square, n_rect):
    group = shards_count * tensor_count
    kind = [2] * n_rect + [1] * n_square + [0] * (group - n_rect - n_square)
    index = list(range(n_rect)) + list(range(n_square)) + [0] * (group - n_rect - n_square)
    return kind, index


def on_device(
    attn_grad,
    mlp_in_grad,
    mlp_out_grad,
    attn_momentum,
    mlp_in_momentum,
    mlp_out_momentum,
    owners,
    embed_weight,
    embed_grad,
    embed_moment,
    embed_second,
    norm_scale,
    norm_partial,
    norm_moment,
    norm_second,
    bias_table,
    bias_partial,
    bias_moment,
    bias_second,
):
    shards_count = lax.axis_size("shards")
    tensor_count = lax.axis_size("tensor")
    group_count = shards_count * tensor_count
    my_index = lax.axis_index(("shards", "tensor"))
    my_row = my_index // tensor_count
    my_col = my_index % tensor_count
    layers_here = owners.shape[0]
    rows_block = attn_grad.shape[2]
    cols_block = attn_grad.shape[3]
    ff_block = mlp_in_grad.shape[3]
    square_width = rows_block * cols_block
    rect_width = rows_block * ff_block
    n_square = layers_here * 4
    n_rect = layers_here * 3
    kind_list, index_list = block_plan(shards_count, tensor_count, n_square, n_rect)
    assert sum(k == 1 for k in kind_list) == n_square and sum(k == 2 for k in kind_list) == n_rect
    kind_table = jnp.array(kind_list, jnp.int32)
    index_table = jnp.array(index_list, jnp.int32)
    square_home = [0] * n_square
    rect_home = [0] * n_rect
    for device, (k, i) in enumerate(zip(kind_list, index_list)):
        if k == 1:
            square_home[i] = device
        elif k == 2:
            rect_home[i] = device

    attn_fresh, attn_ahead = refresh(attn_grad, attn_momentum)
    inner_fresh, inner_ahead = refresh(mlp_in_grad, mlp_in_momentum)
    outer_fresh, outer_ahead = refresh(mlp_out_grad, mlp_out_momentum)
    square_table = jnp.swapaxes(attn_ahead, 2, 3).reshape(n_square, cols_block, rows_block)
    rect_table = jnp.concatenate(
        [jnp.swapaxes(inner_ahead, 2, 3), outer_ahead[:, None]], axis=1
    ).reshape(n_rect, ff_block, rows_block)

    square_ss = jnp.sum(jnp.square(square_table.astype(jnp.float32)), axis=(1, 2))
    rect_ss = jnp.sum(jnp.square(rect_table.astype(jnp.float32)), axis=(1, 2))
    def padded(block):
        return jnp.pad(block, ((0, ff_block - block.shape[0]), (0, 0)))

    bias_flat = bias_partial.reshape(-1)
    bias_across = lax.all_gather(
        jnp.pad(bias_flat, (0, 65536 - bias_flat.shape[0])), "section", axis=0, tiled=False
    )
    bias_sections = jnp.sum(bias_across[:, : bias_flat.shape[0]], axis=0)

    idle_count = group_count - n_rect - n_square
    outgoing = jnp.concatenate(
        [
            rect_table,
            jnp.pad(square_table, ((0, 0), (0, ff_block - cols_block), (0, 0))),
            jnp.zeros((idle_count, ff_block, rows_block), jnp.bfloat16),
        ]
    )
    incoming = lax.all_to_all(outgoing, ("shards", "tensor"), split_axis=0, concat_axis=0, tiled=True)

    norm_partial_late, square_ss, rect_ss, bias_sections, incoming = lax.optimization_barrier(
        (norm_partial, square_ss, rect_ss, bias_sections, incoming)
    )
    norm_width = norm_partial.shape[0] * norm_partial.shape[2]
    bias_width = bias_sections.shape[0]
    packed = jnp.concatenate([norm_partial_late.reshape(norm_width), bias_sections, square_ss, rect_ss])
    packed = jnp.pad(packed, (0, (-packed.shape[0]) % 128))
    gathered_all = lax.all_gather(packed, ("shards", "tensor"), axis=0, tiled=False)

    def run(arrived_blocks, width):
        whole = (
            arrived_blocks[:, :width]
            .reshape(shards_count, tensor_count, width, rows_block)
            .transpose(1, 2, 0, 3)
            .reshape(tensor_count * width, shards_count * rows_block)
        )
        done = newton_schulz_transposed(whole)
        back = (
            done.reshape(tensor_count, width, shards_count, rows_block)
            .transpose(2, 0, 1, 3)
            .reshape(group_count, width, rows_block)
        )
        return jnp.pad(back, ((0, 0), (0, ff_block - width), (0, 0)))

    my_kind = kind_table[my_index]

    def square_branch(arrived_blocks):
        return run(arrived_blocks, cols_block)

    def rect_branch(arrived_blocks):
        return run(arrived_blocks, ff_block)

    def idle_branch(arrived_blocks):
        return jnp.zeros((group_count, ff_block, rows_block), jnp.bfloat16)

    returning = lax.switch(my_kind, [idle_branch, square_branch, rect_branch], incoming)
    returning, gathered_all = lax.optimization_barrier((returning, gathered_all))
    arrived = lax.all_to_all(returning, ("shards", "tensor"), split_axis=0, concat_axis=0, tiled=True)

    gathered = jnp.sum(gathered_all, axis=0)
    norm_grad = gathered[:norm_width].reshape(norm_partial.shape[0], norm_partial.shape[2])
    ss_start = norm_width + bias_width
    square_norm = jnp.sqrt(gathered[ss_start : ss_start + n_square])
    rect_norm = jnp.sqrt(gathered[ss_start + n_square : ss_start + n_square + n_rect])
    bias_grad = gathered[norm_width : norm_width + bias_width].reshape(bias_table.shape)
    rms_all = jnp.concatenate(
        [
            square_norm.reshape(layers_here, 4) / math.sqrt(D * D),
            rect_norm.reshape(layers_here, 3) / math.sqrt(D * FF),
        ],
        axis=1,
    )
    owner_rms = jnp.sum(jnp.where(owners == my_index, rms_all, 0.0)).reshape(1)


    square_rows = jnp.swapaxes(
        jnp.stack([arrived[device, :cols_block] for device in square_home]), 1, 2
    ).reshape(layers_here, 4, rows_block, cols_block).astype(jnp.float32) * (0.2 * math.sqrt(D))
    rect_rows = jnp.stack([arrived[device] for device in rect_home]).reshape(
        layers_here, 3, ff_block, rows_block
    ).astype(jnp.float32) * (0.2 * math.sqrt(FF))
    mlp_in_update = jnp.swapaxes(rect_rows[:, :2], 2, 3)
    mlp_out_update = rect_rows[:, 2]

    embed_results = adamw_update(
        embed_weight, embed_grad.astype(jnp.float32), embed_moment, embed_second, 0.1
    )
    norm_results = adamw_update(norm_scale, norm_grad, norm_moment, norm_second, 0.0)
    bias_results = adamw_update(bias_table, bias_grad, bias_moment, bias_second, 0.0)
    return (
        attn_fresh,
        inner_fresh,
        outer_fresh,
        square_rows,
        mlp_in_update,
        mlp_out_update,
        owner_rms,
        embed_results[0],
        embed_results[1],
        embed_results[2],
        norm_results[0],
        norm_results[1],
        norm_results[2],
        bias_results[0],
        bias_results[1],
        bias_results[2],
    )


def solution(mesh):
    placed = (
        P("section", None, "shards", "tensor"),
        P("section", None, "shards", "tensor"),
        P("section", "tensor", "shards"),
        P("section", None, "shards", "tensor"),
        P("section", None, "shards", "tensor"),
        P("section", "tensor", "shards"),
        P("section", None),
        P(("shards", "tensor", "section"), None),
        P(("shards", "tensor", "section"), None),
        P(("shards", "tensor", "section"), None),
        P(("shards", "tensor", "section"), None),
        P("section", None),
        P("section", ("shards", "tensor"), None),
        P("section", None),
        P("section", None),
        P(),
        P(("shards", "tensor", "section"), None, None),
        P(),
        P(),
    )
    return jax.shard_map(
        on_device,
        mesh=mesh,
        in_specs=placed,
        out_specs=(
            P("section", None, "shards", "tensor"),
            P("section", None, "shards", "tensor"),
            P("section", "tensor", "shards"),
            P("section", None, "shards", "tensor"),
            P("section", None, "shards", "tensor"),
            P("section", "tensor", "shards"),
            P(("shards", "tensor", "section")),
            P(("shards", "tensor", "section"), None),
            P(("shards", "tensor", "section"), None),
            P(("shards", "tensor", "section"), None),
            P("section", None),
            P("section", None),
            P("section", None),
            P(),
            P(),
            P(),
        ),
        check_vma=False,
    )
```

```python
import math

import jax
import jax.numpy as jnp
from jax import lax
from jax.sharding import PartitionSpec as P

D = 1024
FF = 2816
NS_STEPS = 2


coef_first = 3.4445
coef_second = -4.775
coef_third = 2.0315


def newton_schulz_transposed(rows_bf16, norm_value):
    current = (rows_bf16.astype(jnp.float32) / (norm_value + 1e-07)).astype(jnp.bfloat16)
    for sweep_index in range(NS_STEPS):
        gram_form = lax.dot_general(
            current, current, (((0,), (0,)), ((), ())), preferred_element_type=jnp.float32
        ).astype(jnp.bfloat16)
        square_form = jnp.dot(gram_form, gram_form, preferred_element_type=jnp.float32)
        polynomial = (
            coef_second * gram_form.astype(jnp.float32) + coef_third * square_form
        ).astype(jnp.bfloat16)
        current = (
            coef_first * current.astype(jnp.float32)
            + lax.dot_general(
                current, polynomial, (((1,), (1,)), ((), ())), preferred_element_type=jnp.float32
            )
        ).astype(jnp.bfloat16)
    return current


def refresh(gradient, moment):
    fresh_moment = (0.95 * moment.astype(jnp.float32) + gradient.astype(jnp.float32)).astype(
        jnp.bfloat16
    )
    advance = (gradient.astype(jnp.float32) + 0.95 * fresh_moment.astype(jnp.float32)).astype(
        jnp.bfloat16
    )
    return (fresh_moment, advance)


def adamw_update(weight, gradient, moment, second, decay_rate):
    moment_new = 0.9 * moment + 0.1 * gradient
    second_new = 0.95 * second + 0.05 * gradient * gradient
    weight_new = weight - 0.02 * (moment_new / (jnp.sqrt(second_new) + 1e-08) + decay_rate * weight)
    return (weight_new, moment_new, second_new)


def block_plan(shards_count, tensor_count, n_square, n_rect):
    group = shards_count * tensor_count
    kind = [2] * n_rect + [1] * n_square + [0] * (group - n_rect - n_square)
    index = list(range(n_rect)) + list(range(n_square)) + [0] * (group - n_rect - n_square)
    return kind, index


def on_device(
    attn_grad,
    mlp_in_grad,
    mlp_out_grad,
    attn_momentum,
    mlp_in_momentum,
    mlp_out_momentum,
    owners,
    embed_weight,
    embed_grad,
    embed_moment,
    embed_second,
    norm_scale,
    norm_partial,
    norm_moment,
    norm_second,
    bias_table,
    bias_partial,
    bias_moment,
    bias_second,
):
    shards_count = lax.axis_size("shards")
    tensor_count = lax.axis_size("tensor")
    group_count = shards_count * tensor_count
    my_index = lax.axis_index(("shards", "tensor"))
    my_row = my_index // tensor_count
    my_col = my_index % tensor_count
    layers_here = owners.shape[0]
    rows_block = attn_grad.shape[2]
    cols_block = attn_grad.shape[3]
    ff_block = mlp_in_grad.shape[3]
    square_width = rows_block * cols_block
    rect_width = rows_block * ff_block
    n_square = layers_here * 4
    n_rect = layers_here * 3
    kind_list, index_list = block_plan(shards_count, tensor_count, n_square, n_rect)
    assert sum(k == 1 for k in kind_list) == n_square and sum(k == 2 for k in kind_list) == n_rect
    kind_table = jnp.array(kind_list, jnp.int32)
    index_table = jnp.array(index_list, jnp.int32)
    square_home = [0] * n_square
    rect_home = [0] * n_rect
    for device, (k, i) in enumerate(zip(kind_list, index_list)):
        if k == 1:
            square_home[i] = device
        elif k == 2:
            rect_home[i] = device

    attn_fresh, attn_ahead = refresh(attn_grad, attn_momentum)
    inner_fresh, inner_ahead = refresh(mlp_in_grad, mlp_in_momentum)
    outer_fresh, outer_ahead = refresh(mlp_out_grad, mlp_out_momentum)
    square_table = jnp.swapaxes(attn_ahead, 2, 3).reshape(n_square, cols_block, rows_block)
    rect_table = jnp.concatenate(
        [jnp.swapaxes(inner_ahead, 2, 3), outer_ahead[:, None]], axis=1
    ).reshape(n_rect, ff_block, rows_block)

    square_ss = jnp.sum(jnp.square(square_table.astype(jnp.float32)), axis=(1, 2))
    rect_ss = jnp.sum(jnp.square(rect_table.astype(jnp.float32)), axis=(1, 2))
    def padded(block):
        return jnp.pad(block, ((0, ff_block - block.shape[0]), (0, 0)))

    bias_flat = bias_partial.reshape(-1)
    bias_across = lax.all_gather(
        jnp.pad(bias_flat, (0, 65536 - bias_flat.shape[0])), "section", axis=0, tiled=False
    )
    bias_sections = jnp.sum(bias_across[:, : bias_flat.shape[0]], axis=0)

    idle_count = group_count - n_rect - n_square
    outgoing = jnp.concatenate(
        [
            rect_table,
            jnp.pad(square_table, ((0, 0), (0, ff_block - cols_block), (0, 0))),
            jnp.zeros((idle_count, ff_block, rows_block), jnp.bfloat16),
        ]
    )
    incoming = lax.all_to_all(outgoing, ("shards", "tensor"), split_axis=0, concat_axis=0, tiled=True)

    norm_partial_late, square_ss, rect_ss, bias_sections, incoming = lax.optimization_barrier(
        (norm_partial, square_ss, rect_ss, bias_sections, incoming)
    )
    norm_width = norm_partial.shape[0] * norm_partial.shape[2]
    bias_width = bias_sections.shape[0]
    packed = jnp.concatenate([norm_partial_late.reshape(norm_width), bias_sections, square_ss, rect_ss])
    packed = jnp.pad(packed, (0, (-packed.shape[0]) % 128))
    gathered_all = lax.all_gather(packed, ("shards", "tensor"), axis=0, tiled=False)

    def run(arrived_blocks, width):
        whole = (
            arrived_blocks[:, :width]
            .reshape(shards_count, tensor_count, width, rows_block)
            .transpose(1, 2, 0, 3)
            .reshape(tensor_count * width, shards_count * rows_block)
        )
        block_sum = jnp.sum(jnp.square(arrived_blocks.astype(jnp.float32)), axis=0)
        norm_value = jnp.sqrt(jnp.sum(lax.optimization_barrier(block_sum)))
        done = newton_schulz_transposed(whole, norm_value)
        back = (
            done.reshape(tensor_count, width, shards_count, rows_block)
            .transpose(2, 0, 1, 3)
            .reshape(group_count, width, rows_block)
        )
        return jnp.pad(back, ((0, 0), (0, ff_block - width), (0, 0)))

    my_kind = kind_table[my_index]

    def square_branch(arrived_blocks):
        return run(arrived_blocks, cols_block)

    def rect_branch(arrived_blocks):
        return run(arrived_blocks, ff_block)

    def idle_branch(arrived_blocks):
        return jnp.zeros((group_count, ff_block, rows_block), jnp.bfloat16)

    returning = lax.switch(my_kind, [idle_branch, square_branch, rect_branch], incoming)
    returning, gathered_all = lax.optimization_barrier((returning, gathered_all))
    arrived = lax.all_to_all(returning, ("shards", "tensor"), split_axis=0, concat_axis=0, tiled=True)

    gathered = jnp.sum(gathered_all, axis=0)
    norm_grad = gathered[:norm_width].reshape(norm_partial.shape[0], norm_partial.shape[2])
    ss_start = norm_width + bias_width
    square_norm = jnp.sqrt(gathered[ss_start : ss_start + n_square])
    rect_norm = jnp.sqrt(gathered[ss_start + n_square : ss_start + n_square + n_rect])
    bias_grad = gathered[norm_width : norm_width + bias_width].reshape(bias_table.shape)
    rms_all = jnp.concatenate(
        [
            square_norm.reshape(layers_here, 4) / math.sqrt(D * D),
            rect_norm.reshape(layers_here, 3) / math.sqrt(D * FF),
        ],
        axis=1,
    )
    owner_rms = jnp.sum(jnp.where(owners == my_index, rms_all, 0.0)).reshape(1)


    square_rows = jnp.swapaxes(
        jnp.stack([arrived[device, :cols_block] for device in square_home]), 1, 2
    ).reshape(layers_here, 4, rows_block, cols_block).astype(jnp.float32) * (0.2 * math.sqrt(D))
    rect_rows = jnp.stack([arrived[device] for device in rect_home]).reshape(
        layers_here, 3, ff_block, rows_block
    ).astype(jnp.float32) * (0.2 * math.sqrt(FF))
    mlp_in_update = jnp.swapaxes(rect_rows[:, :2], 2, 3)
    mlp_out_update = rect_rows[:, 2]

    embed_results = adamw_update(
        embed_weight, embed_grad.astype(jnp.float32), embed_moment, embed_second, 0.1
    )
    norm_results = adamw_update(norm_scale, norm_grad, norm_moment, norm_second, 0.0)
    bias_results = adamw_update(bias_table, bias_grad, bias_moment, bias_second, 0.0)
    return (
        attn_fresh,
        inner_fresh,
        outer_fresh,
        square_rows,
        mlp_in_update,
        mlp_out_update,
        owner_rms,
        embed_results[0],
        embed_results[1],
        embed_results[2],
        norm_results[0],
        norm_results[1],
        norm_results[2],
        bias_results[0],
        bias_results[1],
        bias_results[2],
    )


def solution(mesh):
    placed = (
        P("section", None, "shards", "tensor"),
        P("section", None, "shards", "tensor"),
        P("section", "tensor", "shards"),
        P("section", None, "shards", "tensor"),
        P("section", None, "shards", "tensor"),
        P("section", "tensor", "shards"),
        P("section", None),
        P(("shards", "tensor", "section"), None),
        P(("shards", "tensor", "section"), None),
        P(("shards", "tensor", "section"), None),
        P(("shards", "tensor", "section"), None),
        P("section", None),
        P("section", ("shards", "tensor"), None),
        P("section", None),
        P("section", None),
        P(),
        P(("shards", "tensor", "section"), None, None),
        P(),
        P(),
    )
    return jax.shard_map(
        on_device,
        mesh=mesh,
        in_specs=placed,
        out_specs=(
            P("section", None, "shards", "tensor"),
            P("section", None, "shards", "tensor"),
            P("section", "tensor", "shards"),
            P("section", None, "shards", "tensor"),
            P("section", None, "shards", "tensor"),
            P("section", "tensor", "shards"),
            P(("shards", "tensor", "section")),
            P(("shards", "tensor", "section"), None),
            P(("shards", "tensor", "section"), None),
            P(("shards", "tensor", "section"), None),
            P("section", None),
            P("section", None),
            P("section", None),
            P(),
            P(),
            P(),
        ),
        check_vma=False,
    )
```

```python
import math

import jax
import jax.numpy as jnp
from jax import lax
from jax.sharding import PartitionSpec as P

D = 1024
FF = 2816
NS_STEPS = 2


coef_first = 3.4445
coef_second = -4.775
coef_third = 2.0315


def newton_schulz_transposed(rows_bf16, norm_value):
    current = (rows_bf16.astype(jnp.float32) / (norm_value + 1e-07)).astype(jnp.bfloat16)
    for sweep_index in range(NS_STEPS):
        gram_form = lax.dot_general(
            current, current, (((0,), (0,)), ((), ())), preferred_element_type=jnp.float32
        ).astype(jnp.bfloat16)
        square_form = jnp.dot(gram_form, gram_form, preferred_element_type=jnp.float32)
        polynomial = (
            coef_second * gram_form.astype(jnp.float32) + coef_third * square_form
        ).astype(jnp.bfloat16)
        current = (
            coef_first * current.astype(jnp.float32)
            + lax.dot_general(
                current, polynomial, (((1,), (1,)), ((), ())), preferred_element_type=jnp.float32
            )
        ).astype(jnp.bfloat16)
    return current


def refresh(gradient, moment):
    fresh_moment = (0.95 * moment.astype(jnp.float32) + gradient.astype(jnp.float32)).astype(
        jnp.bfloat16
    )
    advance = (gradient.astype(jnp.float32) + 0.95 * fresh_moment.astype(jnp.float32)).astype(
        jnp.bfloat16
    )
    return (fresh_moment, advance)


def adamw_update(weight, gradient, moment, second, decay_rate):
    moment_new = 0.9 * moment + 0.1 * gradient
    second_new = 0.95 * second + 0.05 * gradient * gradient
    weight_new = weight - 0.02 * (moment_new / (jnp.sqrt(second_new) + 1e-08) + decay_rate * weight)
    return (weight_new, moment_new, second_new)


def block_plan(shards_count, tensor_count, n_square, n_rect):
    group = shards_count * tensor_count
    kind = [2] * n_rect + [1] * n_square + [0] * (group - n_rect - n_square)
    index = list(range(n_rect)) + list(range(n_square)) + [0] * (group - n_rect - n_square)
    return kind, index


def on_device(
    attn_grad,
    mlp_in_grad,
    mlp_out_grad,
    attn_momentum,
    mlp_in_momentum,
    mlp_out_momentum,
    owners,
    embed_weight,
    embed_grad,
    embed_moment,
    embed_second,
    norm_scale,
    norm_partial,
    norm_moment,
    norm_second,
    bias_table,
    bias_partial,
    bias_moment,
    bias_second,
):
    shards_count = lax.axis_size("shards")
    tensor_count = lax.axis_size("tensor")
    group_count = shards_count * tensor_count
    my_index = lax.axis_index(("shards", "tensor"))
    my_row = my_index // tensor_count
    my_col = my_index % tensor_count
    layers_here = owners.shape[0]
    rows_block = attn_grad.shape[2]
    cols_block = attn_grad.shape[3]
    ff_block = mlp_in_grad.shape[3]
    square_width = rows_block * cols_block
    rect_width = rows_block * ff_block
    n_square = layers_here * 4
    n_rect = layers_here * 3
    kind_list, index_list = block_plan(shards_count, tensor_count, n_square, n_rect)
    assert sum(k == 1 for k in kind_list) == n_square and sum(k == 2 for k in kind_list) == n_rect
    kind_table = jnp.array(kind_list, jnp.int32)
    index_table = jnp.array(index_list, jnp.int32)
    square_home = [0] * n_square
    rect_home = [0] * n_rect
    for device, (k, i) in enumerate(zip(kind_list, index_list)):
        if k == 1:
            square_home[i] = device
        elif k == 2:
            rect_home[i] = device

    attn_fresh, attn_ahead = refresh(attn_grad, attn_momentum)
    inner_fresh, inner_ahead = refresh(mlp_in_grad, mlp_in_momentum)
    outer_fresh, outer_ahead = refresh(mlp_out_grad, mlp_out_momentum)
    square_table = jnp.swapaxes(attn_ahead, 2, 3).reshape(n_square, cols_block, rows_block)
    rect_table = jnp.concatenate(
        [jnp.swapaxes(inner_ahead, 2, 3), outer_ahead[:, None]], axis=1
    ).reshape(n_rect, ff_block, rows_block)

    square_rows_ss, rect_rows_ss = lax.optimization_barrier(
        (
            jnp.sum(jnp.square(square_table.astype(jnp.float32)), axis=1),
            jnp.sum(jnp.square(rect_table.astype(jnp.float32)), axis=1),
        )
    )
    square_ss = jnp.sum(square_rows_ss, axis=1)
    rect_ss = jnp.sum(rect_rows_ss, axis=1)
    def padded(block):
        return jnp.pad(block, ((0, ff_block - block.shape[0]), (0, 0)))

    bias_flat = bias_partial.reshape(-1)
    bias_across = lax.all_gather(
        jnp.pad(bias_flat, (0, 65536 - bias_flat.shape[0])), "section", axis=0, tiled=False
    )
    bias_sections = jnp.sum(bias_across[:, : bias_flat.shape[0]], axis=0)

    idle_count = group_count - n_rect - n_square
    outgoing = jnp.concatenate(
        [
            rect_table,
            jnp.pad(square_table, ((0, 0), (0, ff_block - cols_block), (0, 0))),
            jnp.zeros((idle_count, ff_block, rows_block), jnp.bfloat16),
        ]
    )
    incoming = lax.all_to_all(outgoing, ("shards", "tensor"), split_axis=0, concat_axis=0, tiled=True)

    norm_partial_late, square_ss, rect_ss, bias_sections, incoming = lax.optimization_barrier(
        (norm_partial, square_ss, rect_ss, bias_sections, incoming)
    )
    norm_width = norm_partial.shape[0] * norm_partial.shape[2]
    bias_width = bias_sections.shape[0]
    packed = jnp.concatenate([norm_partial_late.reshape(norm_width), bias_sections, square_ss, rect_ss])
    packed = jnp.pad(packed, (0, (-packed.shape[0]) % 128))
    gathered_all = lax.all_gather(packed, ("shards", "tensor"), axis=0, tiled=False)

    def run(arrived_blocks, width):
        whole = (
            arrived_blocks[:, :width]
            .reshape(shards_count, tensor_count, width, rows_block)
            .transpose(1, 2, 0, 3)
            .reshape(tensor_count * width, shards_count * rows_block)
        )
        block_sum = jnp.sum(jnp.square(arrived_blocks.astype(jnp.float32)), axis=0)
        norm_value = jnp.sqrt(jnp.sum(lax.optimization_barrier(block_sum)))
        done = newton_schulz_transposed(whole, norm_value)
        back = (
            done.reshape(tensor_count, width, shards_count, rows_block)
            .transpose(2, 0, 1, 3)
            .reshape(group_count, width, rows_block)
        )
        return jnp.pad(back, ((0, 0), (0, ff_block - width), (0, 0)))

    my_kind = kind_table[my_index]

    def square_branch(arrived_blocks):
        return run(arrived_blocks, cols_block)

    def rect_branch(arrived_blocks):
        return run(arrived_blocks, ff_block)

    def idle_branch(arrived_blocks):
        return jnp.zeros((group_count, ff_block, rows_block), jnp.bfloat16)

    returning = lax.switch(my_kind, [idle_branch, square_branch, rect_branch], incoming)
    returning, gathered_all = lax.optimization_barrier((returning, gathered_all))
    arrived = lax.all_to_all(returning, ("shards", "tensor"), split_axis=0, concat_axis=0, tiled=True)

    gathered = jnp.sum(gathered_all, axis=0)
    norm_grad = gathered[:norm_width].reshape(norm_partial.shape[0], norm_partial.shape[2])
    ss_start = norm_width + bias_width
    square_norm = jnp.sqrt(gathered[ss_start : ss_start + n_square])
    rect_norm = jnp.sqrt(gathered[ss_start + n_square : ss_start + n_square + n_rect])
    bias_grad = gathered[norm_width : norm_width + bias_width].reshape(bias_table.shape)
    rms_all = jnp.concatenate(
        [
            square_norm.reshape(layers_here, 4) / math.sqrt(D * D),
            rect_norm.reshape(layers_here, 3) / math.sqrt(D * FF),
        ],
        axis=1,
    )
    owner_rms = jnp.sum(jnp.where(owners == my_index, rms_all, 0.0)).reshape(1)


    square_rows = jnp.swapaxes(
        jnp.stack([arrived[device, :cols_block] for device in square_home]), 1, 2
    ).reshape(layers_here, 4, rows_block, cols_block).astype(jnp.float32) * (0.2 * math.sqrt(D))
    rect_rows = jnp.stack([arrived[device] for device in rect_home]).reshape(
        layers_here, 3, ff_block, rows_block
    ).astype(jnp.float32) * (0.2 * math.sqrt(FF))
    mlp_in_update = jnp.swapaxes(rect_rows[:, :2], 2, 3)
    mlp_out_update = rect_rows[:, 2]

    embed_results = adamw_update(
        embed_weight, embed_grad.astype(jnp.float32), embed_moment, embed_second, 0.1
    )
    norm_results = adamw_update(norm_scale, norm_grad, norm_moment, norm_second, 0.0)
    bias_results = adamw_update(bias_table, bias_grad, bias_moment, bias_second, 0.0)
    return (
        attn_fresh,
        inner_fresh,
        outer_fresh,
        square_rows,
        mlp_in_update,
        mlp_out_update,
        owner_rms,
        embed_results[0],
        embed_results[1],
        embed_results[2],
        norm_results[0],
        norm_results[1],
        norm_results[2],
        bias_results[0],
        bias_results[1],
        bias_results[2],
    )


def solution(mesh):
    placed = (
        P("section", None, "shards", "tensor"),
        P("section", None, "shards", "tensor"),
        P("section", "tensor", "shards"),
        P("section", None, "shards", "tensor"),
        P("section", None, "shards", "tensor"),
        P("section", "tensor", "shards"),
        P("section", None),
        P(("shards", "tensor", "section"), None),
        P(("shards", "tensor", "section"), None),
        P(("shards", "tensor", "section"), None),
        P(("shards", "tensor", "section"), None),
        P("section", None),
        P("section", ("shards", "tensor"), None),
        P("section", None),
        P("section", None),
        P(),
        P(("shards", "tensor", "section"), None, None),
        P(),
        P(),
    )
    return jax.shard_map(
        on_device,
        mesh=mesh,
        in_specs=placed,
        out_specs=(
            P("section", None, "shards", "tensor"),
            P("section", None, "shards", "tensor"),
            P("section", "tensor", "shards"),
            P("section", None, "shards", "tensor"),
            P("section", None, "shards", "tensor"),
            P("section", "tensor", "shards"),
            P(("shards", "tensor", "section")),
            P(("shards", "tensor", "section"), None),
            P(("shards", "tensor", "section"), None),
            P(("shards", "tensor", "section"), None),
            P("section", None),
            P("section", None),
            P("section", None),
            P(),
            P(),
            P(),
        ),
        check_vma=False,
    )
```
